256 devices in a mesh: attn: 32 (over z, y), expert: 4 (over x), rep: 2 (over core).
Axes of the slice: x: 4, y: 4, z: 8, core: 2. Of those that a mesh axis runs over, the one named last changes fastest.
Arguments:
- queries: bfloat16 [256, 73728], P('attn', ('expert', 'rep')), may hold values from -120 to 120
- new_latent: bfloat16 [256, 576], P('attn'), may hold values from -6 to 6
- cache_pool: bfloat16 [16384, 576], P('attn'), may hold values from -6 to 6
- local_len: int32 [32, 4], P('attn'), may hold values from 1 to 384, 512 in all within a row
- spill_cache: bfloat16 [1024, 16, 576], P('attn'), may hold values from -6 to 6
- spill_owner: int32 [1024], replicated, may hold values from -1 to 127, as said below
- w_uv: bfloat16 [128, 512, 128], P(('expert', 'rep')), may hold values from -0.25 to 0.25
- w_o: bfloat16 [16384, 7168], P(('expert', 'rep'), 'attn'), may hold values from -0.046875 to 0.046875
- residual: bfloat16 [256, 7168], P(None, 'attn'), may hold values from -3 to 3
- norm_gain: float32 [7168], replicated, may hold values from 0.5 to 1.5
- route_ids: int32 [256, 4], replicated, may hold values from 0 to 15, all different within a row; in each aligned block of 128 rows (0 to 127, 128 to 255, ...) at most 40 rows name the same one
- route_scores: float32 [256, 4], replicated, may hold values from 0.05 to 1
- w_gate: bfloat16 [7168, 32768], P(None, ('attn', 'expert')), may hold values from -0.0625 to 0.0625
- w_up: bfloat16 [7168, 32768], P(None, ('attn', 'expert')), may hold values from -0.0625 to 0.0625
- w_down: bfloat16 [32768, 7168], P(('attn', 'expert')), may hold values from -0.125 to 0.125
Outputs:
- mixed: bfloat16 [256, 7168], P('rep', ('attn', 'expert'))
The draws below stay inside these ranges and needn't reach their ends.
Inputs may be any that keep to these rules, and one draw needn't show every extreme that they name: Each row of local_len sums to 512. `spill_owner`: each entry is -1 or the number of a request that lives on another index of attn than the block's slot. The slots of one index of attn hold at most 2 blocks of the requests of any one other index, and some index holds exactly 2 for some other index in every draw. `route_ids`: the token rows fall into 2 aligned blocks of 128 rows in order (2 being the size of rep); in each block no expert is named by more than 40 rows, and in some block one is named by exactly 40.
All inputs are finite; a program needn't handle non-finite values.
Results may differ from the reference program's by a relative error of at most 0.025.
Values may be sent and summed in bfloat16 or wider, within the bound.
No kernel may reach another device: no remote copies, remote signals or barrier semaphores. Data moves between devices by JAX's collectives and lax.ppermute only.
A program may use at most 128 MiB of HBM per device.

```python
import math
import jax
import jax.numpy as jnp
import numpy as np
from jax import lax

D = 7168
H = 128
LAT = 512
ROPE = 64
VH = 128
FFE = 2048
EXPERTS = 16
TOP = 4
REQ_DEV = 4
POOL = 512
MAXLOC = 384
BLK = 16
CAP = 2
GROUPS = 16
SPILL = 32
TOKENS = 256
CAPJ = 40
N_ATTN = 32
N_REP = 2


def latent_pair(key):
    base_key = jax.random.fold_in(key, 31)
    key_query, key_latent = jax.random.split(base_key, 2)
    row_width = LAT + ROPE
    query_rows = jax.random.truncated_normal(key_query, -6.0, 6.0, (TOKENS, H, row_width), jnp.float32)
    latent = jax.random.truncated_normal(key_latent, -6.0, 6.0, (TOKENS, row_width), jnp.float32)
    return (query_rows.reshape(TOKENS, H * row_width), latent)


def draw_queries(key, part):
    return latent_pair(key)[0].astype(jnp.bfloat16)


def draw_new_latent(key, part):
    return latent_pair(key)[1].astype(jnp.bfloat16)


def draw_spill_owner(key, part):
    base_key = jax.random.fold_in(key, 53)
    key_perm, key_req, key_keep = jax.random.split(base_key, 3)
    permuted = jax.vmap(lambda sub_key: jax.random.permutation(sub_key, N_ATTN - 1))(jax.random.split(key_perm, N_ATTN))
    first_row = permuted[0]
    rolled = (first_row + (N_ATTN - 2) - first_row[0]) % (N_ATTN - 1)
    permuted = permuted.at[0].set(rolled.astype(permuted.dtype))
    offsets = 1 + permuted[:, :GROUPS]
    host_ids = jnp.arange(N_ATTN, dtype=jnp.int32)[:, None]
    owner_dev = (host_ids + offsets) % N_ATTN
    local_req = jax.random.randint(key_req, (N_ATTN, GROUPS, CAP), 0, REQ_DEV)
    local_req = local_req.at[0, 0, 0].set(REQ_DEV - 1)
    kept = jax.random.randint(key_keep, (N_ATTN, GROUPS, CAP), 0, 4) > 0
    forced = (jnp.arange(CAP) == 0)[None, None, :] | (jnp.arange(GROUPS) == 0)[None, :, None]
    kept = kept | forced
    kept = kept.at[0, GROUPS - 1, CAP - 1].set(False)
    owner_ids = jnp.where(kept, owner_dev[:, :, None] * REQ_DEV + local_req, -1)
    return owner_ids.reshape(N_ATTN * GROUPS * CAP).astype(jnp.int32)


def levels(own_key, shape, cuts, least, top_value):
    def one(dim, blocks):
        heights = jax.random.uniform(jax.random.fold_in(jax.random.fold_in(own_key, 6), dim), (blocks,), jnp.float32, least / len(cuts), top_value / len(cuts))
        return jnp.repeat(jnp.exp(heights), shape[dim] // blocks).reshape((-1,) + (1,) * (len(shape) - dim - 1))

    loudness = one(*cuts[0])
    for cut in cuts[1:]:
        loudness = loudness * one(*cut)
    return loudness


def split_up(count, total, reach, lean):
    loads = [(1 << 20) // math.isqrt(grade ** lean) + 1 for grade in range(2, count + 1)]
    spare, given = total - reach - (count - 1), [1] * (count - 1)
    while spare > 0:
        free = [i for i in range(count - 1) if given[i] < reach]
        whole, left = sum([loads[i] for i in free]), spare
        for i in free:
            extra = min(reach - given[i], max(1, left * loads[i] // whole), spare)
            given[i] = given[i] + extra
            spare = spare - extra
    return np.array([reach] + given)


def ragged(own_key, number_of, total, most, slope):
    if number_of == 2:
        one = jax.random.randint(own_key, (), max(1, total - most), min(most, total - 1) + 1)
        return jnp.stack([one, total - one])
    lengths = jnp.asarray(split_up(number_of, total, most, slope), jnp.int32)
    couples = (number_of - 1) // 2
    donor, taker = lengths[1:1 + 2 * couples:2], lengths[2:2 + 2 * couples:2]
    margin = jnp.minimum(donor - 1, most - taker)
    moved = jax.random.randint(jax.random.fold_in(own_key, 1), (couples,), 0, 1 << 20) % (margin + 1)
    lengths = lengths.at[1:1 + 2 * couples:2].set(donor - moved).at[2:2 + 2 * couples:2].set(taker + moved)
    return lengths[jax.random.permutation(jax.random.fold_in(own_key, 2), number_of)]


def routed_block(stream_key, own, number, rows, count, top, most, skew):
    order = jax.random.permutation(stream_key, count)
    heavy_load, ordinary = portions_of(count, rows * top, most, skew, True), portions_of(count, rows * top, most, skew, False)
    places = jnp.arange(count)

    def named(sizes, rotation):
        used = int((sizes > 0).sum())
        fixed = max(1, used // 4)
        moved = fixed + (places - fixed + rotation * (used - fixed)) % max(1, count - fixed)
        return jnp.zeros((count,), jnp.int32).at[order[jnp.where(places < fixed, places, moved)]].set(jnp.asarray(sizes, jnp.int32))

    sizes = jnp.where(number % 4 == 0, named(heavy_load, number // 4), named(ordinary, number - number // 4 - 1))
    mixed = jax.random.permutation(jax.random.fold_in(own, 3), count)
    giver, taker = mixed[0:count // 2 * 2:2], mixed[1:count // 2 * 2:2]
    slack = jnp.minimum(sizes[giver] - 1, most - sizes[taker]) // 2
    slack = jnp.where((giver == order[0]) | (taker == order[0]) | (sizes[taker] == 0), 0, jnp.maximum(slack, 0))
    moved = jax.random.randint(jax.random.fold_in(own, 4), (count // 2,), 0, 1 << 20) % (slack + 1)
    sizes = sizes.at[giver].add(-moved).at[taker].add(moved)
    labels = jnp.searchsorted(jnp.cumsum(sizes), jnp.arange(rows * top), side="right").astype(jnp.int32)
    table = labels.reshape(top, rows).T
    table = table[jax.random.permutation(jax.random.fold_in(own, 1), rows)]
    rotation = jax.random.randint(jax.random.fold_in(own, 2), (rows, 1), 0, top)
    return jnp.take_along_axis(table, (jnp.arange(top)[None, :] + rotation) % top, axis=1)


def portions_of(count, total, limit, slope, full):
    loads = [(1 << 20) // math.isqrt(rank ** slope) + 1 for rank in range(1, count + 1)]
    largest = limit if full else min(limit, max(-(-total // count), total * loads[0] // sum(loads)))
    least = 1 if total - largest >= count - 1 else 0
    counts, rest = [largest] + [least] * (count - 1), total - largest - least * (count - 1)
    while rest > 0:
        movable = [i for i in range(1, count) if counts[i] < largest] or [i for i in range(1, count) if counts[i] < limit]
        whole, budget = sum([loads[i] for i in movable]), rest
        for i in movable:
            more = min(limit - counts[i], max(1, budget * loads[i] // whole), rest)
            counts[i] = counts[i] + more
            rest = rest - more
    return np.array(counts)


def noise(rng, extent, scale, most, cuts=(), kind=jnp.bfloat16):
    values = scale * jax.random.normal(rng, extent, jnp.float32)
    if cuts:
        values = values * levels(rng, extent, cuts, -0.22, 0.18)
    return jnp.clip(values, -most, most).astype(kind)


def setup_inputs(seed: int = 0) -> dict:
    key_list = jax.random.split(jax.random.key(seed), 16)
    queries = draw_queries(jax.random.fold_in(key_list[15], 71), 0)
    new_latent = draw_new_latent(jax.random.fold_in(key_list[15], 71), 0)
    cache_pool = noise(key_list[2], (N_ATTN * POOL, LAT + ROPE), 1.0, 6.0, ((0, 32),))
    local_len = jax.vmap(lambda own: ragged(own, REQ_DEV, POOL, MAXLOC, 2))(jax.random.split(key_list[3], N_ATTN)).reshape((N_ATTN, REQ_DEV)).astype(jnp.int32)
    spill_cache = noise(key_list[4], (N_ATTN * SPILL, BLK, LAT + ROPE), 1.0, 6.0, ((0, 32),))
    spill_owner = draw_spill_owner(jax.random.fold_in(key_list[15], 71), 0)
    w_uv = noise(key_list[6], (H, LAT, VH), LAT ** -0.5, 0.25, ((0, 8),))
    w_o = noise(key_list[7], (H * VH, D), (H * VH) ** -0.5, 0.046875, ((0, 8), (1, 32)))
    residual = noise(key_list[8], (TOKENS, D), 0.5, 3.0, ((1, 32),))
    norm_gain = jnp.clip(1.0 + 0.1 * jax.random.normal(key_list[9], (D,), jnp.float32), 0.5, 1.5)
    route_ids_keys = jax.random.split(jax.random.fold_in(key_list[10], 1), TOKENS // (TOKENS // N_REP))
    route_ids_turns = jax.random.permutation(jax.random.fold_in(key_list[10], 3), TOKENS // (TOKENS // N_REP))
    route_ids = jax.vmap(lambda own, number: routed_block(jax.random.fold_in(key_list[10], 2), own, number, TOKENS // N_REP, EXPERTS, TOP, CAPJ, 1))(route_ids_keys, route_ids_turns).reshape((TOKENS, TOP))
    route_scores = jnp.clip(jnp.exp(jax.random.uniform(key_list[11], (TOKENS, TOP), jnp.float32, math.log(0.05), math.log(1.0))), 0.05, 1.0)
    w_gate = noise(key_list[12], (D, EXPERTS * FFE), D ** -0.5, 0.0625, ((1, 128),))
    w_up = noise(key_list[13], (D, EXPERTS * FFE), D ** -0.5, 0.0625, ((1, 128),))
    w_down = noise(key_list[14], (EXPERTS * FFE, D), FFE ** -0.5, 0.125, ((0, 128),))
    return dict(queries=queries, new_latent=new_latent, cache_pool=cache_pool, local_len=local_len, spill_cache=spill_cache, spill_owner=spill_owner, w_uv=w_uv, w_o=w_o, residual=residual, norm_gain=norm_gain, route_ids=route_ids, route_scores=route_scores, w_gate=w_gate, w_up=w_up, w_down=w_down)


floor_score = -1e+30
scale_out = 2.5

def routed_slots(route_ids):
    row_count = TOKENS // N_REP
    route_part = route_ids.reshape(N_REP, row_count, TOP)
    member = jnp.any(route_part[:, :, :, None] == jnp.arange(EXPERTS, dtype=jnp.int32), axis=2)
    order_rank = (jnp.cumsum(member.astype(jnp.int32), axis=1) - 1).astype(jnp.int32)
    slot_ids = jnp.arange(CAPJ, dtype=jnp.int32)
    slot_hit = member[:, None, :, :] & (order_rank[:, None, :, :] == slot_ids[None, :, None, None])
    place_ids = jnp.arange(row_count, dtype=jnp.int32)
    slot_token = lax.optimization_barrier(jnp.sum(jnp.where(slot_hit, place_ids[None, None, :, None], 0), axis=2)).astype(jnp.int32)
    filled = jnp.any(slot_hit, axis=2)
    offsets = (jnp.arange(N_REP, dtype=jnp.int32) * row_count)[:, None, None]
    return (slot_token + offsets, filled)

def reference(queries, new_latent, cache_pool, local_len, spill_cache, spill_owner, w_uv, w_o, residual, norm_gain, route_ids, route_scores, w_gate, w_up, w_down):
    score_scale = float(VH + ROPE) ** (-0.5)
    row_width = LAT + ROPE
    requests = N_ATTN * REQ_DEV
    query_rows = queries.reshape(requests, 2, H, row_width).astype(jnp.float32)
    pools = jnp.concatenate([cache_pool.reshape(N_ATTN, POOL, row_width), jnp.zeros((N_ATTN, MAXLOC, row_width), cache_pool.dtype)], axis=1)
    starts = (jnp.cumsum(local_len, axis=1) - local_len).astype(jnp.int32)

    def device_windows(pool_rows, start_row):
        return jax.vmap(lambda start_one: lax.dynamic_slice_in_dim(pool_rows, start_one, MAXLOC, 0))(start_row)
    windows = jax.vmap(device_windows)(pools, starts).reshape(requests, MAXLOC, row_width).astype(jnp.float32)
    local_scores = jnp.einsum('rthc,rkc->rthk', query_rows, windows) * score_scale
    inside = jnp.arange(MAXLOC, dtype=jnp.int32)[None, :] < local_len.reshape(requests)[:, None]
    local_scores = jnp.where(inside[:, None, None, :], local_scores, floor_score)
    fresh_keys = new_latent.reshape(requests, 2, row_width).astype(jnp.float32)
    fresh_scores = jnp.einsum('rthc,rkc->rthk', query_rows, fresh_keys) * score_scale
    causal = jnp.arange(2)[None, :] <= jnp.arange(2)[:, None]
    fresh_scores = jnp.where(causal[None, :, None, :], fresh_scores, floor_score)
    present = spill_owner >= 0
    owner_ids = jnp.where(present, spill_owner, 0).astype(jnp.int32)
    spill_rows = spill_cache.astype(jnp.float32)
    slot_query = query_rows[owner_ids]
    spill_scores = jnp.einsum('nthc,nbc->nthb', slot_query, spill_rows) * score_scale
    spill_scores = jnp.where(present[:, None, None, None], spill_scores, floor_score)
    row_top = jnp.maximum(lax.optimization_barrier(jnp.max(local_scores, axis=3)), lax.optimization_barrier(jnp.max(fresh_scores, axis=3)))
    row_top = row_top.at[owner_ids].max(lax.optimization_barrier(jnp.max(spill_scores, axis=3)))
    local_weight = jnp.exp(local_scores - row_top[..., None])
    fresh_weight = jnp.exp(fresh_scores - row_top[..., None])
    spill_weight = jnp.exp(spill_scores - row_top[owner_ids][..., None])
    spill_weight = jnp.where(present[:, None, None, None], spill_weight, 0.0)
    denominator = lax.optimization_barrier(jnp.sum(local_weight, axis=3)) + lax.optimization_barrier(jnp.sum(fresh_weight, axis=3))
    denominator = denominator.at[owner_ids].add(lax.optimization_barrier(jnp.sum(spill_weight, axis=3)))
    numerator = jnp.einsum('rthk,rkc->rthc', local_weight.astype(jnp.bfloat16).astype(jnp.float32), windows[:, :, :LAT])
    numerator = numerator + jnp.einsum('rthk,rkc->rthc', fresh_weight.astype(jnp.bfloat16).astype(jnp.float32), fresh_keys[:, :, :LAT])
    spill_numer = jnp.einsum('nthb,nbc->nthc', spill_weight.astype(jnp.bfloat16).astype(jnp.float32), spill_rows[:, :, :LAT])
    numerator = numerator.at[owner_ids].add(spill_numer)
    attended = (numerator / denominator[..., None]).astype(jnp.bfloat16)
    values = jnp.einsum('rthc,hcv->rthv', attended.astype(jnp.float32), w_uv.astype(jnp.float32)).astype(jnp.bfloat16)
    values = values.reshape(TOKENS, H * VH)
    hidden = (residual.astype(jnp.float32) + jnp.dot(values, w_o, preferred_element_type=jnp.float32)).astype(jnp.bfloat16)
    widened = hidden.astype(jnp.float32)
    normed = (widened * lax.rsqrt(lax.optimization_barrier(jnp.mean(widened * widened, axis=1, keepdims=True)) + 1e-06) * norm_gain).astype(jnp.bfloat16)
    share = route_scores / lax.optimization_barrier(jnp.sum(route_scores, axis=1, keepdims=True))
    share_table = lax.optimization_barrier(jnp.sum(jnp.where(route_ids[:, :, None] == jnp.arange(EXPERTS, dtype=jnp.int32), share[:, :, None], 0.0), axis=1))
    slot_token, filled = routed_slots(route_ids)

    def expert_out(expert_index):
        row_ids = slot_token[:, :, expert_index].reshape(-1)
        row_ok = filled[:, :, expert_index].reshape(-1)
        picked = normed[row_ids]
        gate_proj = jnp.dot(picked, lax.dynamic_slice_in_dim(w_gate, expert_index * FFE, FFE, 1), preferred_element_type=jnp.float32)
        up_proj = jnp.dot(picked, lax.dynamic_slice_in_dim(w_up, expert_index * FFE, FFE, 1), preferred_element_type=jnp.float32)
        activated = (jax.nn.silu(gate_proj) * up_proj).astype(jnp.bfloat16)
        result = jnp.dot(activated, lax.dynamic_slice_in_dim(w_down, expert_index * FFE, FFE, 0), preferred_element_type=jnp.float32)
        weight_coef = jnp.where(row_ok, share_table[row_ids, expert_index], 0.0) * scale_out
        return weight_coef[:, None] * result
    outputs = lax.map(expert_out, jnp.arange(EXPERTS, dtype=jnp.int32))
    all_rows = jnp.transpose(slot_token, (2, 0, 1)).reshape(-1)
    routed = jnp.zeros((TOKENS, D), jnp.float32).at[all_rows].add(outputs.reshape(-1, D))
    return (hidden.astype(jnp.float32) + routed).astype(jnp.bfloat16)
```

```python
import jax
import jax.numpy as jnp
from jax import lax
from jax.sharding import PartitionSpec as P

ROPE = 64
VH = 128
EXPERTS = 16
TOP = 4
CAP = 2


floor_score = -1e30
scale_out = 2.5
HIGH = lax.Precision.HIGHEST


def expert_tables(route_ids, part_index, part_count, capacity):
    row_count = route_ids.shape[0] // part_count
    route_part = lax.dynamic_slice_in_dim(route_ids, part_index * row_count, row_count, 0)
    member = jnp.any(
        route_part[:, :, None] == jnp.arange(EXPERTS, dtype=jnp.int32)[None, None, :], axis=1
    )
    order_rank = jnp.cumsum(member.astype(jnp.int32), axis=0) - 1
    slot_ids = jnp.arange(capacity, dtype=jnp.int32)
    pick = (member.T[:, None, :]) & (order_rank.T[:, None, :] == slot_ids[None, :, None])
    return pick, route_part


def per_device(
    queries,
    new_latent,
    cache_pool,
    local_len,
    spill_cache,
    spill_owner,
    w_uv,
    w_o,
    residual,
    norm_gain,
    route_ids,
    route_scores,
    w_gate,
    w_up,
    w_down,
):
    n_attn = lax.axis_size("attn")
    n_expert = lax.axis_size("expert")
    n_rep = lax.axis_size("rep")
    attn_here = lax.axis_index("attn")
    expert_here = lax.axis_index("expert")
    rep_here = lax.axis_index("rep")
    req_count = local_len.shape[1]
    head_count = w_uv.shape[0]
    row_width = new_latent.shape[1]
    lat_width = w_uv.shape[1]
    pool_rows = cache_pool.shape[0]
    score_scale = float(VH + ROPE) ** (-0.5)

    spill_count = spill_cache.shape[0]
    blk = spill_cache.shape[1]
    directory = spill_owner.reshape(n_attn, spill_count)
    owner_dev = jnp.where(directory >= 0, directory // req_count, -1)
    earlier = jnp.arange(spill_count)[:, None] > jnp.arange(spill_count)[None, :]
    same_owner = owner_dev[:, :, None] == owner_dev[:, None, :]
    order_rank = jnp.sum(same_owner & earlier[None, :, :], axis=2)
    slot_ids = jnp.arange(CAP)
    own_row = owner_dev[attn_here]
    own_rank = order_rank[attn_here]
    pick_slot = (own_row[None, None, :] == jnp.arange(n_attn)[:, None, None]) & (
        own_rank[None, None, :] == slot_ids[None, :, None]
    )
    outgoing = jnp.einsum(
        "dks,sbc->dkbc",
        pick_slot.astype(jnp.bfloat16),
        spill_cache,
        preferred_element_type=jnp.float32,
    ).astype(jnp.bfloat16)
    incoming = lax.all_to_all(outgoing, "attn", split_axis=0, concat_axis=0, tiled=True)
    mine_slot = (owner_dev[:, None, :] == attn_here) & (
        order_rank[:, None, :] == slot_ids[None, :, None]
    )
    present = jnp.any(mine_slot, axis=2).reshape(-1)
    request = jnp.sum(
        jnp.where(mine_slot, directory[:, None, :] - attn_here * req_count, 0), axis=2
    ).reshape(-1)
    spill_rows = incoming.reshape(n_attn * CAP * blk, row_width)

    query_rows = queries.reshape(req_count, 2, head_count, row_width)
    lengths = local_len[0]
    starts = jnp.cumsum(lengths) - lengths
    pos = jnp.arange(pool_rows)
    pool_ok = (pos[None, :] >= starts[:, None]) & (pos[None, :] < (starts + lengths)[:, None])
    pool_scores = (
        jnp.einsum("rthc,kc->rthk", query_rows, cache_pool, preferred_element_type=jnp.float32)
        * score_scale
    )
    pool_scores = jnp.where(pool_ok[:, None, None, :], pool_scores, floor_score)
    fresh_scores = (
        jnp.einsum("rthc,kc->rthk", query_rows, new_latent, preferred_element_type=jnp.float32)
        * score_scale
    )
    fresh_pos = jnp.arange(2 * req_count)
    fresh_ok = (fresh_pos[None, None, :] // 2 == jnp.arange(req_count)[:, None, None]) & (
        fresh_pos[None, None, :] % 2 <= jnp.arange(2)[None, :, None]
    )
    fresh_scores = jnp.where(fresh_ok[:, :, None, :], fresh_scores, floor_score)
    block_ok = (request[None, :] == jnp.arange(req_count)[:, None]) & present[None, :]
    spill_ok = jnp.broadcast_to(block_ok[:, :, None], block_ok.shape + (blk,)).reshape(
        req_count, -1
    )
    spill_scores = (
        jnp.einsum("rthc,kc->rthk", query_rows, spill_rows, preferred_element_type=jnp.float32)
        * score_scale
    )
    spill_scores = jnp.where(spill_ok[:, None, None, :], spill_scores, floor_score)
    row_top = jnp.maximum(
        jnp.maximum(jnp.max(pool_scores, axis=3), jnp.max(fresh_scores, axis=3)),
        jnp.max(spill_scores, axis=3),
    )
    pool_weight = jnp.exp(pool_scores - row_top[..., None])
    fresh_weight = jnp.exp(fresh_scores - row_top[..., None])
    spill_weight = jnp.exp(spill_scores - row_top[..., None])
    denominator = (
        jnp.sum(pool_weight, axis=3) + jnp.sum(fresh_weight, axis=3) + jnp.sum(spill_weight, axis=3)
    )
    numerator = jnp.einsum(
        "rthk,kc->rthc",
        pool_weight.astype(jnp.bfloat16),
        cache_pool[:, :lat_width],
        preferred_element_type=jnp.float32,
    )
    numerator = numerator + jnp.einsum(
        "rthk,kc->rthc",
        fresh_weight.astype(jnp.bfloat16),
        new_latent[:, :lat_width],
        preferred_element_type=jnp.float32,
    )
    numerator = numerator + jnp.einsum(
        "rthk,kc->rthc",
        spill_weight.astype(jnp.bfloat16),
        spill_rows[:, :lat_width],
        preferred_element_type=jnp.float32,
    )
    attended = (numerator / denominator[..., None]).astype(jnp.bfloat16)
    values = jnp.einsum(
        "rthc,hcv->rthv", attended, w_uv, preferred_element_type=jnp.float32
    ).astype(jnp.bfloat16)
    tok_here = 2 * req_count
    values = values.reshape(tok_here, head_count * w_uv.shape[2])

    spread = jnp.broadcast_to(values[None], (n_attn,) + values.shape)
    all_values = lax.all_to_all(spread, "attn", split_axis=0, concat_axis=0, tiled=True)
    all_values = all_values.reshape(n_attn * tok_here, -1)
    partial_cols = jnp.dot(all_values, w_o, preferred_element_type=jnp.float32)

    tokens = partial_cols.shape[0]
    rows_part = tokens // n_rep
    sub_cols = partial_cols.shape[1] // n_expert
    pieces = (
        partial_cols.astype(jnp.bfloat16)
        .reshape(n_rep, rows_part, n_expert, sub_cols)
        .transpose(2, 0, 1, 3)
        .reshape(n_expert * n_rep, rows_part, sub_cols)
    )
    got = lax.all_to_all(pieces, ("expert", "rep"), split_axis=0, concat_axis=0, tiled=True)
    attn_own = jnp.sum(got.astype(jnp.float32), axis=0)
    res_own = lax.dynamic_slice(
        residual, (rep_here * rows_part, expert_here * sub_cols), (rows_part, sub_cols)
    )
    hidden_own = (res_own.astype(jnp.float32) + attn_own).astype(jnp.bfloat16)

    capacity = rows_part * TOP // EXPERTS * 5 // 4
    shards = n_attn * n_expert // EXPERTS
    pick, route_part = expert_tables(route_ids, rep_here, n_rep, capacity)
    pick_f = pick.astype(jnp.float32)
    rows_e = jnp.einsum(
        "jsr,rc->jsc", pick.astype(jnp.bfloat16), hidden_own, preferred_element_type=jnp.float32
    ).astype(jnp.bfloat16)
    send_rows = jnp.repeat(rows_e, shards, axis=0)
    recv_rows = lax.all_to_all(send_rows, ("attn", "expert"), split_axis=0, concat_axis=0, tiled=True)
    full_rows = recv_rows.transpose(1, 0, 2).reshape(capacity, -1)
    widened = full_rows.astype(jnp.float32)
    normed = (
        widened * lax.rsqrt(jnp.mean(widened * widened, axis=1, keepdims=True) + 1e-06) * norm_gain
    ).astype(jnp.bfloat16)
    gate_proj = jnp.dot(normed, w_gate, preferred_element_type=jnp.float32)
    up_proj = jnp.dot(normed, w_up, preferred_element_type=jnp.float32)
    activated = (jax.nn.silu(gate_proj) * up_proj).astype(jnp.bfloat16)
    result = jnp.dot(activated, w_down, preferred_element_type=jnp.float32)

    n_dev = n_attn * n_expert
    back = result.astype(jnp.bfloat16).reshape(capacity, n_dev, sub_cols).transpose(1, 0, 2)
    returned = lax.all_to_all(back, ("attn", "expert"), split_axis=0, concat_axis=0, tiled=True)
    summed = jnp.sum(
        returned.astype(jnp.float32).reshape(EXPERTS, shards, capacity, sub_cols), axis=1
    )
    share_part = lax.dynamic_slice_in_dim(route_scores, rep_here * rows_part, rows_part, 0)
    share_part = share_part / jnp.sum(share_part, axis=1, keepdims=True)
    share_table = jnp.sum(
        jnp.where(
            route_part[:, :, None] == jnp.arange(EXPERTS, dtype=jnp.int32)[None, None, :],
            share_part[:, :, None],
            0.0,
        ),
        axis=1,
    )
    coef = jnp.sum(jnp.where(pick, share_table.T[:, None, :], 0.0), axis=2) * scale_out
    weighted = coef[:, :, None] * summed
    routed = jnp.einsum("jsr,jsc->rc", pick_f, weighted, precision=HIGH)
    return (hidden_own.astype(jnp.float32) + routed).astype(jnp.bfloat16)


def solution(mesh):
    return jax.shard_map(
        per_device,
        mesh=mesh,
        in_specs=(
            P("attn", ("expert", "rep")),
            P("attn", None),
            P("attn", None),
            P("attn", None),
            P("attn", None, None),
            P(),
            P(("expert", "rep"), None, None),
            P(("expert", "rep"), "attn"),
            P(None, "attn"),
            P(),
            P(),
            P(),
            P(None, ("attn", "expert")),
            P(None, ("attn", "expert")),
            P(("attn", "expert"), None),
        ),
        out_specs=P("rep", ("attn", "expert")),
        check_vma=False,
    )
```

```python
import jax
import jax.numpy as jnp
from jax import lax
from jax.sharding import PartitionSpec as P

ROPE = 64
VH = 128
EXPERTS = 16
TOP = 4
CAP = 2


floor_score = -1e30
scale_out = 2.5
HIGH = lax.Precision.HIGHEST


def expert_tables(route_ids, part_index, part_count, capacity):
    row_count = route_ids.shape[0] // part_count
    route_part = lax.dynamic_slice_in_dim(route_ids, part_index * row_count, row_count, 0)
    member = jnp.any(
        route_part[:, :, None] == jnp.arange(EXPERTS, dtype=jnp.int32)[None, None, :], axis=1
    )
    order_rank = jnp.cumsum(member.astype(jnp.int32), axis=0) - 1
    slot_ids = jnp.arange(capacity, dtype=jnp.int32)
    pick = (member.T[:, None, :]) & (order_rank.T[:, None, :] == slot_ids[None, :, None])
    return pick, route_part


def per_device(
    queries,
    new_latent,
    cache_pool,
    local_len,
    spill_cache,
    spill_owner,
    w_uv,
    w_o,
    residual,
    norm_gain,
    route_ids,
    route_scores,
    w_gate,
    w_up,
    w_down,
):
    n_attn = lax.axis_size("attn")
    n_expert = lax.axis_size("expert")
    n_rep = lax.axis_size("rep")
    attn_here = lax.axis_index("attn")
    expert_here = lax.axis_index("expert")
    rep_here = lax.axis_index("rep")
    req_count = local_len.shape[1]
    head_count = w_uv.shape[0]
    row_width = new_latent.shape[1]
    lat_width = w_uv.shape[1]
    pool_rows = cache_pool.shape[0]
    score_scale = float(VH + ROPE) ** (-0.5)

    spill_count = spill_cache.shape[0]
    blk = spill_cache.shape[1]
    directory = spill_owner.reshape(n_attn, spill_count)
    owner_dev = jnp.where(directory >= 0, directory // req_count, -1)
    earlier = jnp.arange(spill_count)[:, None] > jnp.arange(spill_count)[None, :]
    same_owner = owner_dev[:, :, None] == owner_dev[:, None, :]
    order_rank = jnp.sum(same_owner & earlier[None, :, :], axis=2)
    slot_ids = jnp.arange(CAP)
    own_row = owner_dev[attn_here]
    own_rank = order_rank[attn_here]
    pick_slot = (own_row[None, None, :] == jnp.arange(n_attn)[:, None, None]) & (
        own_rank[None, None, :] == slot_ids[None, :, None]
    )
    my_slot = lax.dynamic_slice_in_dim(pick_slot, rep_here, 1, 1)
    outgoing = jnp.einsum(
        "dks,sbc->dkbc",
        my_slot.astype(jnp.bfloat16),
        spill_cache,
        preferred_element_type=jnp.float32,
    ).astype(jnp.bfloat16)
    half = lax.all_to_all(outgoing, "attn", split_axis=0, concat_axis=0, tiled=True)
    other = lax.ppermute(half, "rep", [(i, (i + 1) % n_rep) for i in range(n_rep)])
    first = jnp.where(rep_here == 0, half, other)
    second = jnp.where(rep_here == 0, other, half)
    incoming = jnp.concatenate([first, second], axis=1)
    mine_slot = (owner_dev[:, None, :] == attn_here) & (
        order_rank[:, None, :] == slot_ids[None, :, None]
    )
    present = jnp.any(mine_slot, axis=2).reshape(-1)
    request = jnp.sum(
        jnp.where(mine_slot, directory[:, None, :] - attn_here * req_count, 0), axis=2
    ).reshape(-1)
    spill_rows = incoming.reshape(n_attn * CAP * blk, row_width)

    query_rows = queries.reshape(req_count, 2, head_count, row_width)
    lengths = local_len[0]
    starts = jnp.cumsum(lengths) - lengths
    pos = jnp.arange(pool_rows)
    pool_ok = (pos[None, :] >= starts[:, None]) & (pos[None, :] < (starts + lengths)[:, None])
    pool_scores = (
        jnp.einsum("rthc,kc->rthk", query_rows, cache_pool, preferred_element_type=jnp.float32)
        * score_scale
    )
    pool_scores = jnp.where(pool_ok[:, None, None, :], pool_scores, floor_score)
    fresh_scores = (
        jnp.einsum("rthc,kc->rthk", query_rows, new_latent, preferred_element_type=jnp.float32)
        * score_scale
    )
    fresh_pos = jnp.arange(2 * req_count)
    fresh_ok = (fresh_pos[None, None, :] // 2 == jnp.arange(req_count)[:, None, None]) & (
        fresh_pos[None, None, :] % 2 <= jnp.arange(2)[None, :, None]
    )
    fresh_scores = jnp.where(fresh_ok[:, :, None, :], fresh_scores, floor_score)
    block_ok = (request[None, :] == jnp.arange(req_count)[:, None]) & present[None, :]
    spill_ok = jnp.broadcast_to(block_ok[:, :, None], block_ok.shape + (blk,)).reshape(
        req_count, -1
    )
    spill_scores = (
        jnp.einsum("rthc,kc->rthk", query_rows, spill_rows, preferred_element_type=jnp.float32)
        * score_scale
    )
    spill_scores = jnp.where(spill_ok[:, None, None, :], spill_scores, floor_score)
    row_top = jnp.maximum(
        jnp.maximum(jnp.max(pool_scores, axis=3), jnp.max(fresh_scores, axis=3)),
        jnp.max(spill_scores, axis=3),
    )
    pool_weight = jnp.exp(pool_scores - row_top[..., None])
    fresh_weight = jnp.exp(fresh_scores - row_top[..., None])
    spill_weight = jnp.exp(spill_scores - row_top[..., None])
    denominator = (
        jnp.sum(pool_weight, axis=3) + jnp.sum(fresh_weight, axis=3) + jnp.sum(spill_weight, axis=3)
    )
    numerator = jnp.einsum(
        "rthk,kc->rthc",
        pool_weight.astype(jnp.bfloat16),
        cache_pool[:, :lat_width],
        preferred_element_type=jnp.float32,
    )
    numerator = numerator + jnp.einsum(
        "rthk,kc->rthc",
        fresh_weight.astype(jnp.bfloat16),
        new_latent[:, :lat_width],
        preferred_element_type=jnp.float32,
    )
    numerator = numerator + jnp.einsum(
        "rthk,kc->rthc",
        spill_weight.astype(jnp.bfloat16),
        spill_rows[:, :lat_width],
        preferred_element_type=jnp.float32,
    )
    attended = (numerator / denominator[..., None]).astype(jnp.bfloat16)
    values = jnp.einsum(
        "rthc,hcv->rthv", attended, w_uv, preferred_element_type=jnp.float32
    ).astype(jnp.bfloat16)
    tok_here = 2 * req_count
    values = values.reshape(tok_here, head_count * w_uv.shape[2])

    spread = jnp.broadcast_to(values[None], (n_attn,) + values.shape)
    all_values = lax.all_to_all(spread, "attn", split_axis=0, concat_axis=0, tiled=True)
    all_values = all_values.reshape(n_attn * tok_here, -1)
    partial_cols = jnp.dot(all_values, w_o, preferred_element_type=jnp.float32)

    tokens = partial_cols.shape[0]
    rows_part = tokens // n_rep
    sub_cols = partial_cols.shape[1] // n_expert
    pieces = (
        partial_cols.astype(jnp.bfloat16)
        .reshape(n_rep, rows_part, n_expert, sub_cols)
        .transpose(2, 0, 1, 3)
        .reshape(n_expert * n_rep, rows_part, sub_cols)
    )
    got = lax.all_to_all(pieces, ("expert", "rep"), split_axis=0, concat_axis=0, tiled=True)
    attn_own = jnp.sum(got.astype(jnp.float32), axis=0)
    res_own = lax.dynamic_slice(
        residual, (rep_here * rows_part, expert_here * sub_cols), (rows_part, sub_cols)
    )
    hidden_own = (res_own.astype(jnp.float32) + attn_own).astype(jnp.bfloat16)

    capacity = rows_part * TOP // EXPERTS * 5 // 4
    shards = n_attn * n_expert // EXPERTS
    pick, route_part = expert_tables(route_ids, rep_here, n_rep, capacity)
    pick_f = pick.astype(jnp.float32)
    rows_e = jnp.einsum(
        "jsr,rc->jsc", pick.astype(jnp.bfloat16), hidden_own, preferred_element_type=jnp.float32
    ).astype(jnp.bfloat16)
    send_rows = jnp.repeat(rows_e, shards, axis=0)
    recv_rows = lax.all_to_all(send_rows, ("attn", "expert"), split_axis=0, concat_axis=0, tiled=True)
    full_rows = recv_rows.transpose(1, 0, 2).reshape(capacity, -1)
    widened = full_rows.astype(jnp.float32)
    normed = (
        widened * lax.rsqrt(jnp.mean(widened * widened, axis=1, keepdims=True) + 1e-06) * norm_gain
    ).astype(jnp.bfloat16)
    gate_proj = jnp.dot(normed, w_gate, preferred_element_type=jnp.float32)
    up_proj = jnp.dot(normed, w_up, preferred_element_type=jnp.float32)
    activated = (jax.nn.silu(gate_proj) * up_proj).astype(jnp.bfloat16)
    result = jnp.dot(activated, w_down, preferred_element_type=jnp.float32)

    n_dev = n_attn * n_expert
    back = result.astype(jnp.bfloat16).reshape(capacity, n_dev, sub_cols).transpose(1, 0, 2)
    returned = lax.all_to_all(back, ("attn", "expert"), split_axis=0, concat_axis=0, tiled=True)
    summed = jnp.sum(
        returned.astype(jnp.float32).reshape(EXPERTS, shards, capacity, sub_cols), axis=1
    )
    share_part = lax.dynamic_slice_in_dim(route_scores, rep_here * rows_part, rows_part, 0)
    share_part = share_part / jnp.sum(share_part, axis=1, keepdims=True)
    share_table = jnp.sum(
        jnp.where(
            route_part[:, :, None] == jnp.arange(EXPERTS, dtype=jnp.int32)[None, None, :],
            share_part[:, :, None],
            0.0,
        ),
        axis=1,
    )
    coef = jnp.sum(jnp.where(pick, share_table.T[:, None, :], 0.0), axis=2) * scale_out
    weighted = coef[:, :, None] * summed
    routed = jnp.einsum("jsr,jsc->rc", pick_f, weighted, precision=HIGH)
    return (hidden_own.astype(jnp.float32) + routed).astype(jnp.bfloat16)


def solution(mesh):
    return jax.shard_map(
        per_device,
        mesh=mesh,
        in_specs=(
            P("attn", ("expert", "rep")),
            P("attn", None),
            P("attn", None),
            P("attn", None),
            P("attn", None, None),
            P(),
            P(("expert", "rep"), None, None),
            P(("expert", "rep"), "attn"),
            P(None, "attn"),
            P(),
            P(),
            P(),
            P(None, ("attn", "expert")),
            P(None, ("attn", "expert")),
            P(("attn", "expert"), None),
        ),
        out_specs=P("rep", ("attn", "expert")),
        check_vma=False,
    )
```

```python
import jax
import jax.numpy as jnp
from jax import lax
from jax.sharding import PartitionSpec as P

ROPE = 64
VH = 128
EXPERTS = 16
TOP = 4
CAP = 2


floor_score = -1e30
scale_out = 2.5
HIGH = lax.Precision.HIGHEST


def expert_tables(route_ids, part_index, part_count, capacity):
    row_count = route_ids.shape[0] // part_count
    route_part = lax.dynamic_slice_in_dim(route_ids, part_index * row_count, row_count, 0)
    member = jnp.any(
        route_part[:, :, None] == jnp.arange(EXPERTS, dtype=jnp.int32)[None, None, :], axis=1
    )
    order_rank = jnp.cumsum(member.astype(jnp.int32), axis=0) - 1
    slot_ids = jnp.arange(capacity, dtype=jnp.int32)
    pick = (member.T[:, None, :]) & (order_rank.T[:, None, :] == slot_ids[None, :, None])
    return pick, route_part


def per_device(
    queries,
    new_latent,
    cache_pool,
    local_len,
    spill_cache,
    spill_owner,
    w_uv,
    w_o,
    residual,
    norm_gain,
    route_ids,
    route_scores,
    w_gate,
    w_up,
    w_down,
):
    n_attn = lax.axis_size("attn")
    n_expert = lax.axis_size("expert")
    n_rep = lax.axis_size("rep")
    attn_here = lax.axis_index("attn")
    expert_here = lax.axis_index("expert")
    rep_here = lax.axis_index("rep")
    req_count = local_len.shape[1]
    head_count = w_uv.shape[0]
    row_width = new_latent.shape[1]
    lat_width = w_uv.shape[1]
    pool_rows = cache_pool.shape[0]
    score_scale = float(VH + ROPE) ** (-0.5)

    spill_count = spill_cache.shape[0]
    blk = spill_cache.shape[1]
    directory = spill_owner.reshape(n_attn, spill_count)
    owner_dev = jnp.where(directory >= 0, directory // req_count, -1)
    earlier = jnp.arange(spill_count)[:, None] > jnp.arange(spill_count)[None, :]
    same_owner = owner_dev[:, :, None] == owner_dev[:, None, :]
    order_rank = jnp.sum(same_owner & earlier[None, :, :], axis=2)
    slot_ids = jnp.arange(CAP)
    own_row = owner_dev[attn_here]
    own_rank = order_rank[attn_here]
    pick_slot = (own_row[None, None, :] == jnp.arange(n_attn)[:, None, None]) & (
        own_rank[None, None, :] == slot_ids[None, :, None]
    )
    my_slot = lax.dynamic_slice_in_dim(pick_slot, rep_here, 1, 1)
    outgoing = jnp.einsum(
        "dks,sbc->dkbc",
        my_slot.astype(jnp.bfloat16),
        spill_cache,
        preferred_element_type=jnp.float32,
    ).astype(jnp.bfloat16)
    half = lax.all_to_all(outgoing, "attn", split_axis=0, concat_axis=0, tiled=True)
    other = lax.ppermute(half, "rep", [(i, (i + 1) % n_rep) for i in range(n_rep)])
    first = jnp.where(rep_here == 0, half, other)
    second = jnp.where(rep_here == 0, other, half)
    incoming = jnp.concatenate([first, second], axis=1)
    mine_slot = (owner_dev[:, None, :] == attn_here) & (
        order_rank[:, None, :] == slot_ids[None, :, None]
    )
    present = jnp.any(mine_slot, axis=2).reshape(-1)
    request = jnp.sum(
        jnp.where(mine_slot, directory[:, None, :] - attn_here * req_count, 0), axis=2
    ).reshape(-1)
    spill_rows = incoming.reshape(n_attn * CAP * blk, row_width)

    query_rows = queries.reshape(req_count, 2, head_count, row_width)
    lengths = local_len[0]
    starts = jnp.cumsum(lengths) - lengths
    pos = jnp.arange(pool_rows)
    pool_ok = (pos[None, :] >= starts[:, None]) & (pos[None, :] < (starts + lengths)[:, None])
    pool_scores = (
        jnp.einsum("rthc,kc->rthk", query_rows, cache_pool, preferred_element_type=jnp.float32)
        * score_scale
    )
    pool_scores = jnp.where(pool_ok[:, None, None, :], pool_scores, floor_score)
    fresh_scores = (
        jnp.einsum("rthc,kc->rthk", query_rows, new_latent, preferred_element_type=jnp.float32)
        * score_scale
    )
    fresh_pos = jnp.arange(2 * req_count)
    fresh_ok = (fresh_pos[None, None, :] // 2 == jnp.arange(req_count)[:, None, None]) & (
        fresh_pos[None, None, :] % 2 <= jnp.arange(2)[None, :, None]
    )
    fresh_scores = jnp.where(fresh_ok[:, :, None, :], fresh_scores, floor_score)
    block_ok = (request[None, :] == jnp.arange(req_count)[:, None]) & present[None, :]
    spill_ok = jnp.broadcast_to(block_ok[:, :, None], block_ok.shape + (blk,)).reshape(
        req_count, -1
    )
    spill_scores = (
        jnp.einsum("rthc,kc->rthk", query_rows, spill_rows, preferred_element_type=jnp.float32)
        * score_scale
    )
    spill_scores = jnp.where(spill_ok[:, None, None, :], spill_scores, floor_score)
    row_top = jnp.maximum(
        jnp.maximum(jnp.max(pool_scores, axis=3), jnp.max(fresh_scores, axis=3)),
        jnp.max(spill_scores, axis=3),
    )
    pool_weight = jnp.exp(pool_scores - row_top[..., None])
    fresh_weight = jnp.exp(fresh_scores - row_top[..., None])
    spill_weight = jnp.exp(spill_scores - row_top[..., None])
    denominator = (
        jnp.sum(pool_weight, axis=3) + jnp.sum(fresh_weight, axis=3) + jnp.sum(spill_weight, axis=3)
    )
    numerator = jnp.einsum(
        "rthk,kc->rthc",
        pool_weight.astype(jnp.bfloat16),
        cache_pool[:, :lat_width],
        preferred_element_type=jnp.float32,
    )
    numerator = numerator + jnp.einsum(
        "rthk,kc->rthc",
        fresh_weight.astype(jnp.bfloat16),
        new_latent[:, :lat_width],
        preferred_element_type=jnp.float32,
    )
    numerator = numerator + jnp.einsum(
        "rthk,kc->rthc",
        spill_weight.astype(jnp.bfloat16),
        spill_rows[:, :lat_width],
        preferred_element_type=jnp.float32,
    )
    attended = (numerator / denominator[..., None]).astype(jnp.bfloat16)
    values = jnp.einsum(
        "rthc,hcv->rthv", attended, w_uv, preferred_element_type=jnp.float32
    ).astype(jnp.bfloat16)
    tok_here = 2 * req_count
    values = values.reshape(tok_here, head_count * w_uv.shape[2])

    spread = jnp.broadcast_to(values[None], (n_attn,) + values.shape)
    all_values = lax.all_to_all(spread, "attn", split_axis=0, concat_axis=0, tiled=True)
    all_values = all_values.reshape(n_attn * tok_here, -1)
    partial_cols = jnp.dot(all_values, w_o, preferred_element_type=jnp.float32)

    tokens = partial_cols.shape[0]
    rows_part = tokens // n_rep
    sub_cols = partial_cols.shape[1] // n_expert
    pieces = (
        partial_cols.astype(jnp.bfloat16)
        .reshape(n_rep, rows_part, n_expert, sub_cols)
        .transpose(2, 0, 1, 3)
        .reshape(n_expert * n_rep, rows_part, sub_cols)
    )
    got = lax.all_to_all(pieces, ("expert", "rep"), split_axis=0, concat_axis=0, tiled=True)
    attn_own = jnp.sum(got.astype(jnp.float32), axis=0)
    res_own = lax.dynamic_slice(
        residual, (rep_here * rows_part, expert_here * sub_cols), (rows_part, sub_cols)
    )
    hidden_own = (res_own.astype(jnp.float32) + attn_own).astype(jnp.bfloat16)

    capacity = rows_part * TOP // EXPERTS * 5 // 4
    shards = n_attn * n_expert // EXPERTS
    pick, route_part = expert_tables(route_ids, rep_here, n_rep, capacity)
    pick_f = pick.astype(jnp.float32)
    rows_e = jnp.einsum(
        "jsr,rc->jsc", pick.astype(jnp.bfloat16), hidden_own, preferred_element_type=jnp.float32
    ).astype(jnp.bfloat16)
    send_rows = jnp.repeat(rows_e, shards, axis=0)
    recv_rows = lax.all_to_all(send_rows, ("attn", "expert"), split_axis=0, concat_axis=0, tiled=True)
    full_rows = recv_rows.transpose(1, 0, 2).reshape(capacity, -1)
    widened = full_rows.astype(jnp.float32)
    normed = (
        widened * lax.rsqrt(jnp.mean(widened * widened, axis=1, keepdims=True) + 1e-06) * norm_gain
    ).astype(jnp.bfloat16)
    gate_proj = jnp.dot(normed, w_gate, preferred_element_type=jnp.float32)
    up_proj = jnp.dot(normed, w_up, preferred_element_type=jnp.float32)
    activated = (jax.nn.silu(gate_proj) * up_proj).astype(jnp.bfloat16)
    n_dev = n_attn * n_expert
    down_blocks = w_down.reshape(w_down.shape[0], n_dev, sub_cols).transpose(1, 0, 2)
    back = jnp.einsum(
        "ku,duc->dkc", activated, down_blocks, preferred_element_type=jnp.float32
    ).astype(jnp.bfloat16)
    returned = lax.all_to_all(back, ("attn", "expert"), split_axis=0, concat_axis=0, tiled=True)
    summed = jnp.sum(
        returned.astype(jnp.float32).reshape(EXPERTS, shards, capacity, sub_cols), axis=1
    )
    share_part = lax.dynamic_slice_in_dim(route_scores, rep_here * rows_part, rows_part, 0)
    share_part = share_part / jnp.sum(share_part, axis=1, keepdims=True)
    share_table = jnp.sum(
        jnp.where(
            route_part[:, :, None] == jnp.arange(EXPERTS, dtype=jnp.int32)[None, None, :],
            share_part[:, :, None],
            0.0,
        ),
        axis=1,
    )
    coef = jnp.sum(jnp.where(pick, share_table.T[:, None, :], 0.0), axis=2) * scale_out
    weighted = coef[:, :, None] * summed
    routed = jnp.einsum("jsr,jsc->rc", pick_f, weighted, precision=HIGH)
    return (hidden_own.astype(jnp.float32) + routed).astype(jnp.bfloat16)


def solution(mesh):
    return jax.shard_map(
        per_device,
        mesh=mesh,
        in_specs=(
            P("attn", ("expert", "rep")),
            P("attn", None),
            P("attn", None),
            P("attn", None),
            P("attn", None, None),
            P(),
            P(("expert", "rep"), None, None),
            P(("expert", "rep"), "attn"),
            P(None, "attn"),
            P(),
            P(),
            P(),
            P(None, ("attn", "expert")),
            P(None, ("attn", "expert")),
            P(("attn", "expert"), None),
        ),
        out_specs=P("rep", ("attn", "expert")),
        check_vma=False,
    )
```

```python
import jax
import jax.numpy as jnp
from jax import lax
from jax.sharding import PartitionSpec as P

ROPE = 64
VH = 128
EXPERTS = 16
TOP = 4
CAP = 2


floor_score = -1e30
scale_out = 2.5
HIGH = lax.Precision.HIGHEST


def expert_tables(route_ids, part_index, part_count, capacity):
    row_count = route_ids.shape[0] // part_count
    route_part = lax.dynamic_slice_in_dim(route_ids, part_index * row_count, row_count, 0)
    member = jnp.any(
        route_part[:, :, None] == jnp.arange(EXPERTS, dtype=jnp.int32)[None, None, :], axis=1
    )
    order_rank = jnp.cumsum(member.astype(jnp.int32), axis=0) - 1
    slot_ids = jnp.arange(capacity, dtype=jnp.int32)
    pick = (member.T[:, None, :]) & (order_rank.T[:, None, :] == slot_ids[None, :, None])
    return pick, route_part


def per_device(
    queries,
    new_latent,
    cache_pool,
    local_len,
    spill_cache,
    spill_owner,
    w_uv,
    w_o,
    residual,
    norm_gain,
    route_ids,
    route_scores,
    w_gate,
    w_up,
    w_down,
):
    n_attn = lax.axis_size("attn")
    n_expert = lax.axis_size("expert")
    n_rep = lax.axis_size("rep")
    attn_here = lax.axis_index("attn")
    expert_here = lax.axis_index("expert")
    rep_here = lax.axis_index("rep")
    req_count = local_len.shape[1]
    head_count = w_uv.shape[0]
    row_width = new_latent.shape[1]
    lat_width = w_uv.shape[1]
    pool_rows = cache_pool.shape[0]
    score_scale = float(VH + ROPE) ** (-0.5)

    spill_count = spill_cache.shape[0]
    blk = spill_cache.shape[1]
    directory = spill_owner.reshape(n_attn, spill_count)
    owner_dev = jnp.where(directory >= 0, directory // req_count, -1)
    earlier = jnp.arange(spill_count)[:, None] > jnp.arange(spill_count)[None, :]
    same_owner = owner_dev[:, :, None] == owner_dev[:, None, :]
    order_rank = jnp.sum(same_owner & earlier[None, :, :], axis=2)
    slot_ids = jnp.arange(CAP)
    own_row = owner_dev[attn_here]
    own_rank = order_rank[attn_here]
    pick_slot = (own_row[None, None, :] == jnp.arange(n_attn)[:, None, None]) & (
        own_rank[None, None, :] == slot_ids[None, :, None]
    )
    my_slot = lax.dynamic_slice_in_dim(pick_slot, rep_here, 1, 1)
    outgoing = jnp.einsum(
        "dks,sbc->dkbc",
        my_slot.astype(jnp.bfloat16),
        spill_cache,
        preferred_element_type=jnp.float32,
    ).astype(jnp.bfloat16)
    half = lax.all_to_all(outgoing, "attn", split_axis=0, concat_axis=0, tiled=True)
    other = lax.ppermute(half, "rep", [(i, (i + 1) % n_rep) for i in range(n_rep)])
    first = jnp.where(rep_here == 0, half, other)
    second = jnp.where(rep_here == 0, other, half)
    incoming = jnp.concatenate([first, second], axis=1)
    mine_slot = (owner_dev[:, None, :] == attn_here) & (
        order_rank[:, None, :] == slot_ids[None, :, None]
    )
    present = jnp.any(mine_slot, axis=2).reshape(-1)
    request = jnp.sum(
        jnp.where(mine_slot, directory[:, None, :] - attn_here * req_count, 0), axis=2
    ).reshape(-1)
    spill_rows = incoming.reshape(n_attn * CAP * blk, row_width)

    query_rows = queries.reshape(req_count, 2, head_count, row_width)
    lengths = local_len[0]
    starts = jnp.cumsum(lengths) - lengths
    pos = jnp.arange(pool_rows)
    pool_ok = (pos[None, :] >= starts[:, None]) & (pos[None, :] < (starts + lengths)[:, None])
    pool_scores = (
        jnp.einsum("rthc,kc->rthk", query_rows, cache_pool, preferred_element_type=jnp.float32)
        * score_scale
    )
    pool_scores = jnp.where(pool_ok[:, None, None, :], pool_scores, floor_score)
    fresh_scores = (
        jnp.einsum("rthc,kc->rthk", query_rows, new_latent, preferred_element_type=jnp.float32)
        * score_scale
    )
    fresh_pos = jnp.arange(2 * req_count)
    fresh_ok = (fresh_pos[None, None, :] // 2 == jnp.arange(req_count)[:, None, None]) & (
        fresh_pos[None, None, :] % 2 <= jnp.arange(2)[None, :, None]
    )
    fresh_scores = jnp.where(fresh_ok[:, :, None, :], fresh_scores, floor_score)
    block_ok = (request[None, :] == jnp.arange(req_count)[:, None]) & present[None, :]
    spill_ok = jnp.broadcast_to(block_ok[:, :, None], block_ok.shape + (blk,)).reshape(
        req_count, -1
    )
    spill_scores = (
        jnp.einsum("rthc,kc->rthk", query_rows, spill_rows, preferred_element_type=jnp.float32)
        * score_scale
    )
    spill_scores = jnp.where(spill_ok[:, None, None, :], spill_scores, floor_score)
    row_top = jnp.maximum(
        jnp.maximum(jnp.max(pool_scores, axis=3), jnp.max(fresh_scores, axis=3)),
        jnp.max(spill_scores, axis=3),
    )
    pool_weight = jnp.exp(pool_scores - row_top[..., None])
    fresh_weight = jnp.exp(fresh_scores - row_top[..., None])
    spill_weight = jnp.exp(spill_scores - row_top[..., None])
    denominator = (
        jnp.sum(pool_weight, axis=3) + jnp.sum(fresh_weight, axis=3) + jnp.sum(spill_weight, axis=3)
    )
    numerator = jnp.einsum(
        "rthk,kc->rthc",
        pool_weight.astype(jnp.bfloat16),
        cache_pool[:, :lat_width],
        preferred_element_type=jnp.float32,
    )
    numerator = numerator + jnp.einsum(
        "rthk,kc->rthc",
        fresh_weight.astype(jnp.bfloat16),
        new_latent[:, :lat_width],
        preferred_element_type=jnp.float32,
    )
    numerator = numerator + jnp.einsum(
        "rthk,kc->rthc",
        spill_weight.astype(jnp.bfloat16),
        spill_rows[:, :lat_width],
        preferred_element_type=jnp.float32,
    )
    attended = (numerator / denominator[..., None]).astype(jnp.bfloat16)
    values = jnp.einsum(
        "rthc,hcv->rthv", attended, w_uv, preferred_element_type=jnp.float32
    ).astype(jnp.bfloat16)
    tok_here = 2 * req_count
    values = values.reshape(tok_here, head_count * w_uv.shape[2])

    spread = jnp.broadcast_to(values[None], (n_attn,) + values.shape)
    all_values = lax.all_to_all(spread, "attn", split_axis=0, concat_axis=0, tiled=True)
    all_values = all_values.reshape(n_attn * tok_here, -1)
    partial_cols = jnp.dot(all_values, w_o, preferred_element_type=jnp.float32)

    tokens = partial_cols.shape[0]
    rows_part = tokens // n_rep
    sub_cols = partial_cols.shape[1] // n_expert
    pieces = (
        partial_cols.astype(jnp.bfloat16)
        .reshape(n_rep, rows_part, n_expert, sub_cols)
        .transpose(2, 0, 1, 3)
        .reshape(n_expert * n_rep, rows_part, sub_cols)
    )
    got = lax.all_to_all(pieces, ("expert", "rep"), split_axis=0, concat_axis=0, tiled=True)
    attn_own = jnp.sum(got.astype(jnp.float32), axis=0)
    res_own = lax.dynamic_slice(
        residual, (rep_here * rows_part, expert_here * sub_cols), (rows_part, sub_cols)
    )
    hidden_own = (res_own.astype(jnp.float32) + attn_own).astype(jnp.bfloat16)

    capacity = rows_part * TOP // EXPERTS * 5 // 4
    shards = n_attn * n_expert // EXPERTS
    pick, route_part = expert_tables(route_ids, rep_here, n_rep, capacity)
    pick_f = pick.astype(jnp.float32)
    rows_e = jnp.einsum(
        "jsr,rc->jsc", pick.astype(jnp.bfloat16), hidden_own, preferred_element_type=jnp.float32
    ).astype(jnp.bfloat16)
    send_rows = jnp.repeat(rows_e, shards, axis=0)
    recv_rows = lax.all_to_all(send_rows, ("attn", "expert"), split_axis=0, concat_axis=0, tiled=True)
    n_src = recv_rows.shape[0]
    widened = recv_rows.astype(jnp.float32)
    mean_sq = jnp.sum(widened * widened, axis=(0, 2)) / (n_src * sub_cols)
    inv = lax.rsqrt(mean_sq + 1e-06)
    normed = (
        widened * inv[None, :, None] * norm_gain.reshape(n_src, 1, sub_cols)
    ).astype(jnp.bfloat16)
    gate_blocks = w_gate.reshape(n_src, sub_cols, w_gate.shape[1])
    up_blocks = w_up.reshape(n_src, sub_cols, w_up.shape[1])
    gate_proj = jnp.einsum("skc,scu->ku", normed, gate_blocks, preferred_element_type=jnp.float32)
    up_proj = jnp.einsum("skc,scu->ku", normed, up_blocks, preferred_element_type=jnp.float32)
    activated = (jax.nn.silu(gate_proj) * up_proj).astype(jnp.bfloat16)
    n_dev = n_attn * n_expert
    down_blocks = w_down.reshape(w_down.shape[0], n_dev, sub_cols).transpose(1, 0, 2)
    back = jnp.einsum(
        "ku,duc->dkc", activated, down_blocks, preferred_element_type=jnp.float32
    ).astype(jnp.bfloat16)
    returned = lax.all_to_all(back, ("attn", "expert"), split_axis=0, concat_axis=0, tiled=True)
    summed = jnp.sum(
        returned.astype(jnp.float32).reshape(EXPERTS, shards, capacity, sub_cols), axis=1
    )
    share_part = lax.dynamic_slice_in_dim(route_scores, rep_here * rows_part, rows_part, 0)
    share_part = share_part / jnp.sum(share_part, axis=1, keepdims=True)
    share_table = jnp.sum(
        jnp.where(
            route_part[:, :, None] == jnp.arange(EXPERTS, dtype=jnp.int32)[None, None, :],
            share_part[:, :, None],
            0.0,
        ),
        axis=1,
    )
    coef = jnp.sum(jnp.where(pick, share_table.T[:, None, :], 0.0), axis=2) * scale_out
    weighted = coef[:, :, None] * summed
    routed = jnp.einsum("jsr,jsc->rc", pick_f, weighted, precision=HIGH)
    return (hidden_own.astype(jnp.float32) + routed).astype(jnp.bfloat16)


def solution(mesh):
    return jax.shard_map(
        per_device,
        mesh=mesh,
        in_specs=(
            P("attn", ("expert", "rep")),
            P("attn", None),
            P("attn", None),
            P("attn", None),
            P("attn", None, None),
            P(),
            P(("expert", "rep"), None, None),
            P(("expert", "rep"), "attn"),
            P(None, "attn"),
            P(),
            P(),
            P(),
            P(None, ("attn", "expert")),
            P(None, ("attn", "expert")),
            P(("attn", "expert"), None),
        ),
        out_specs=P("rep", ("attn", "expert")),
        check_vma=False,
    )
```

```python
import jax
import jax.numpy as jnp
from jax import lax
from jax.sharding import PartitionSpec as P

ROPE = 64
VH = 128
EXPERTS = 16
TOP = 4
CAP = 2


floor_score = -1e30
scale_out = 2.5
HIGH = lax.Precision.HIGHEST


def expert_tables(route_ids, part_index, part_count, capacity):
    row_count = route_ids.shape[0] // part_count
    route_part = lax.dynamic_slice_in_dim(route_ids, part_index * row_count, row_count, 0)
    member = jnp.any(
        route_part[:, :, None] == jnp.arange(EXPERTS, dtype=jnp.int32)[None, None, :], axis=1
    )
    order_rank = jnp.cumsum(member.astype(jnp.int32), axis=0) - 1
    slot_ids = jnp.arange(capacity, dtype=jnp.int32)
    pick = (member.T[:, None, :]) & (order_rank.T[:, None, :] == slot_ids[None, :, None])
    return pick, route_part


def per_device(
    queries,
    new_latent,
    cache_pool,
    local_len,
    spill_cache,
    spill_owner,
    w_uv,
    w_o,
    residual,
    norm_gain,
    route_ids,
    route_scores,
    w_gate,
    w_up,
    w_down,
):
    n_attn = lax.axis_size("attn")
    n_expert = lax.axis_size("expert")
    n_rep = lax.axis_size("rep")
    attn_here = lax.axis_index("attn")
    expert_here = lax.axis_index("expert")
    rep_here = lax.axis_index("rep")
    req_count = local_len.shape[1]
    head_count = w_uv.shape[0]
    row_width = new_latent.shape[1]
    lat_width = w_uv.shape[1]
    pool_rows = cache_pool.shape[0]
    score_scale = float(VH + ROPE) ** (-0.5)

    spill_count = spill_cache.shape[0]
    blk = spill_cache.shape[1]
    earlier = jnp.arange(spill_count)[:, None] > jnp.arange(spill_count)[None, :]
    own_ids = lax.dynamic_slice_in_dim(spill_owner, attn_here * spill_count, spill_count, 0)
    own_row = jnp.where(own_ids >= 0, own_ids // req_count, -1)
    own_rank = jnp.sum((own_row[:, None] == own_row[None, :]) & earlier, axis=1)
    my_slot = (own_row[None, :] == jnp.arange(n_attn)[:, None]) & (own_rank == rep_here)[None, :]
    outgoing = jnp.einsum(
        "ds,sbc->dbc",
        my_slot.astype(jnp.bfloat16),
        spill_cache,
        preferred_element_type=jnp.float32,
    ).astype(jnp.bfloat16)[:, None]
    half = lax.all_to_all(outgoing, "attn", split_axis=0, concat_axis=0, tiled=True)
    directory = spill_owner.reshape(n_attn, spill_count)
    owner_dev = jnp.where(directory >= 0, directory // req_count, -1)
    same_owner = owner_dev[:, :, None] == owner_dev[:, None, :]
    order_rank = jnp.sum(same_owner & earlier[None, :, :], axis=2)
    other = lax.ppermute(half, "rep", [(i, (i + 1) % n_rep) for i in range(n_rep)])
    part_slots = jnp.stack([rep_here, n_rep - 1 - rep_here])
    mine_slot = (owner_dev[:, None, :] == attn_here) & (
        order_rank[:, None, :] == part_slots[None, :, None]
    )
    present = jnp.any(mine_slot, axis=2)
    request = jnp.sum(
        jnp.where(mine_slot, directory[:, None, :] - attn_here * req_count, 0), axis=2
    )
    spill_parts = [part.reshape(n_attn * blk, row_width) for part in (half, other)]

    query_rows = queries.reshape(req_count, 2, head_count, row_width)
    lengths = local_len[0]
    starts = jnp.cumsum(lengths) - lengths
    pos = jnp.arange(pool_rows)
    pool_ok = (pos[None, :] >= starts[:, None]) & (pos[None, :] < (starts + lengths)[:, None])
    pool_scores = (
        jnp.einsum("rthc,kc->rthk", query_rows, cache_pool, preferred_element_type=jnp.float32)
        * score_scale
    )
    pool_scores = jnp.where(pool_ok[:, None, None, :], pool_scores, floor_score)
    fresh_scores = (
        jnp.einsum("rthc,kc->rthk", query_rows, new_latent, preferred_element_type=jnp.float32)
        * score_scale
    )
    fresh_pos = jnp.arange(2 * req_count)
    fresh_ok = (fresh_pos[None, None, :] // 2 == jnp.arange(req_count)[:, None, None]) & (
        fresh_pos[None, None, :] % 2 <= jnp.arange(2)[None, :, None]
    )
    fresh_scores = jnp.where(fresh_ok[:, :, None, :], fresh_scores, floor_score)
    row_top = jnp.maximum(jnp.max(pool_scores, axis=3), jnp.max(fresh_scores, axis=3))
    spill_scores = []
    for part_index, part_rows in enumerate(spill_parts):
        block_ok = (request[None, :, part_index] == jnp.arange(req_count)[:, None]) & present[
            None, :, part_index
        ]
        spill_ok = jnp.broadcast_to(block_ok[:, :, None], block_ok.shape + (blk,)).reshape(
            req_count, -1
        )
        part_scores = (
            jnp.einsum("rthc,kc->rthk", query_rows, part_rows, preferred_element_type=jnp.float32)
            * score_scale
        )
        part_scores = jnp.where(spill_ok[:, None, None, :], part_scores, floor_score)
        row_top = jnp.maximum(row_top, jnp.max(part_scores, axis=3))
        spill_scores.append(part_scores)
    pool_weight = jnp.exp(pool_scores - row_top[..., None])
    fresh_weight = jnp.exp(fresh_scores - row_top[..., None])
    spill_weight = [jnp.exp(part - row_top[..., None]) for part in spill_scores]
    denominator = jnp.sum(pool_weight, axis=3) + jnp.sum(fresh_weight, axis=3)
    for part in spill_weight:
        denominator = denominator + jnp.sum(part, axis=3)
    numerator = jnp.einsum(
        "rthk,kc->rthc",
        pool_weight.astype(jnp.bfloat16),
        cache_pool[:, :lat_width],
        preferred_element_type=jnp.float32,
    )
    numerator = numerator + jnp.einsum(
        "rthk,kc->rthc",
        fresh_weight.astype(jnp.bfloat16),
        new_latent[:, :lat_width],
        preferred_element_type=jnp.float32,
    )
    for part, part_rows in zip(spill_weight, spill_parts):
        numerator = numerator + jnp.einsum(
            "rthk,kc->rthc",
            part.astype(jnp.bfloat16),
            part_rows[:, :lat_width],
            preferred_element_type=jnp.float32,
        )
    attended = (numerator / denominator[..., None]).astype(jnp.bfloat16)
    values = jnp.einsum(
        "rthc,hcv->rthv", attended, w_uv, preferred_element_type=jnp.float32
    ).astype(jnp.bfloat16)
    tok_here = 2 * req_count
    values = values.reshape(tok_here, head_count * w_uv.shape[2])

    spread = jnp.broadcast_to(values[None], (n_attn,) + values.shape)
    all_values = lax.all_to_all(spread, "attn", split_axis=0, concat_axis=0, tiled=True)
    all_values = all_values.reshape(n_attn * tok_here, -1)
    partial_cols = jnp.dot(all_values, w_o, preferred_element_type=jnp.float32)

    tokens = partial_cols.shape[0]
    rows_part = tokens // n_rep
    sub_cols = partial_cols.shape[1] // n_expert
    pieces = (
        partial_cols.astype(jnp.bfloat16)
        .reshape(n_rep, rows_part, n_expert, sub_cols)
        .transpose(2, 0, 1, 3)
        .reshape(n_expert * n_rep, rows_part, sub_cols)
    )
    got = lax.all_to_all(pieces, ("expert", "rep"), split_axis=0, concat_axis=0, tiled=True)
    attn_own = jnp.sum(got.astype(jnp.float32), axis=0)
    res_own = lax.dynamic_slice(
        residual, (rep_here * rows_part, expert_here * sub_cols), (rows_part, sub_cols)
    )
    hidden_own = (res_own.astype(jnp.float32) + attn_own).astype(jnp.bfloat16)

    capacity = rows_part * TOP // EXPERTS * 5 // 4
    shards = n_attn * n_expert // EXPERTS
    pick, route_part = expert_tables(route_ids, rep_here, n_rep, capacity)
    pick_f = pick.astype(jnp.float32)
    rows_e = jnp.einsum(
        "jsr,rc->jsc", pick.astype(jnp.bfloat16), hidden_own, preferred_element_type=jnp.float32
    ).astype(jnp.bfloat16)
    send_rows = jnp.repeat(rows_e, shards, axis=0)
    recv_rows = lax.all_to_all(send_rows, ("attn", "expert"), split_axis=0, concat_axis=0, tiled=True)
    n_src = recv_rows.shape[0]
    widened = recv_rows.astype(jnp.float32)
    mean_sq = jnp.sum(widened * widened, axis=(0, 2)) / (n_src * sub_cols)
    inv = lax.rsqrt(mean_sq + 1e-06)
    normed = (
        widened * inv[None, :, None] * norm_gain.reshape(n_src, 1, sub_cols)
    ).astype(jnp.bfloat16)
    gate_blocks = w_gate.reshape(n_src, sub_cols, w_gate.shape[1])
    up_blocks = w_up.reshape(n_src, sub_cols, w_up.shape[1])
    gate_proj = jnp.einsum("skc,scu->ku", normed, gate_blocks, preferred_element_type=jnp.float32)
    up_proj = jnp.einsum("skc,scu->ku", normed, up_blocks, preferred_element_type=jnp.float32)
    activated = (jax.nn.silu(gate_proj) * up_proj).astype(jnp.bfloat16)
    n_dev = n_attn * n_expert
    down_blocks = w_down.reshape(w_down.shape[0], n_dev, sub_cols).transpose(1, 0, 2)
    back = jnp.einsum(
        "ku,duc->dkc", activated, down_blocks, preferred_element_type=jnp.float32
    ).astype(jnp.bfloat16)
    returned = lax.all_to_all(back, ("attn", "expert"), split_axis=0, concat_axis=0, tiled=True)
    summed = jnp.sum(
        returned.astype(jnp.float32).reshape(EXPERTS, shards, capacity, sub_cols), axis=1
    )
    share_part = lax.dynamic_slice_in_dim(route_scores, rep_here * rows_part, rows_part, 0)
    share_part = share_part / jnp.sum(share_part, axis=1, keepdims=True)
    share_table = jnp.sum(
        jnp.where(
            route_part[:, :, None] == jnp.arange(EXPERTS, dtype=jnp.int32)[None, None, :],
            share_part[:, :, None],
            0.0,
        ),
        axis=1,
    )
    coef = jnp.sum(jnp.where(pick, share_table.T[:, None, :], 0.0), axis=2) * scale_out
    weighted = coef[:, :, None] * summed
    routed = jnp.einsum("jsr,jsc->rc", pick_f, weighted, precision=HIGH)
    return (hidden_own.astype(jnp.float32) + routed).astype(jnp.bfloat16)


def solution(mesh):
    return jax.shard_map(
        per_device,
        mesh=mesh,
        in_specs=(
            P("attn", ("expert", "rep")),
            P("attn", None),
            P("attn", None),
            P("attn", None),
            P("attn", None, None),
            P(),
            P(("expert", "rep"), None, None),
            P(("expert", "rep"), "attn"),
            P(None, "attn"),
            P(),
            P(),
            P(),
            P(None, ("attn", "expert")),
            P(None, ("attn", "expert")),
            P(("attn", "expert"), None),
        ),
        out_specs=P("rep", ("attn", "expert")),
        check_vma=False,
    )
```

```python
import jax
import jax.numpy as jnp
from jax import lax
from jax.sharding import PartitionSpec as P

ROPE = 64
VH = 128
EXPERTS = 16
TOP = 4
CAP = 2


floor_score = -1e30
scale_out = 2.5
HIGH = lax.Precision.HIGHEST


def expert_tables(route_ids, part_index, part_count, capacity):
    row_count = route_ids.shape[0] // part_count
    route_part = lax.dynamic_slice_in_dim(route_ids, part_index * row_count, row_count, 0)
    member = jnp.any(
        route_part[:, :, None] == jnp.arange(EXPERTS, dtype=jnp.int32)[None, None, :], axis=1
    )
    order_rank = jnp.cumsum(member.astype(jnp.int32), axis=0) - 1
    slot_ids = jnp.arange(capacity, dtype=jnp.int32)
    pick = (member.T[:, None, :]) & (order_rank.T[:, None, :] == slot_ids[None, :, None])
    return pick, route_part


def per_device(
    queries,
    new_latent,
    cache_pool,
    local_len,
    spill_cache,
    spill_owner,
    w_uv,
    w_o,
    residual,
    norm_gain,
    route_ids,
    route_scores,
    w_gate,
    w_up,
    w_down,
):
    n_attn = lax.axis_size("attn")
    n_expert = lax.axis_size("expert")
    n_rep = lax.axis_size("rep")
    attn_here = lax.axis_index("attn")
    expert_here = lax.axis_index("expert")
    rep_here = lax.axis_index("rep")
    req_count = local_len.shape[1]
    head_count = w_uv.shape[0]
    row_width = new_latent.shape[1]
    lat_width = w_uv.shape[1]
    pool_rows = cache_pool.shape[0]
    score_scale = float(VH + ROPE) ** (-0.5)

    spill_count = spill_cache.shape[0]
    blk = spill_cache.shape[1]
    directory = spill_owner.reshape(n_attn, spill_count)
    owner_dev = jnp.where(directory >= 0, directory // req_count, -1)
    earlier = jnp.arange(spill_count)[:, None] > jnp.arange(spill_count)[None, :]
    same_owner = owner_dev[:, :, None] == owner_dev[:, None, :]
    order_rank = jnp.sum(same_owner & earlier[None, :, :], axis=2)
    slot_ids = jnp.arange(CAP)
    own_row = owner_dev[attn_here]
    own_rank = order_rank[attn_here]
    pick_slot = (own_row[None, None, :] == jnp.arange(n_attn)[:, None, None]) & (
        own_rank[None, None, :] == slot_ids[None, :, None]
    )
    my_slot = lax.dynamic_slice_in_dim(pick_slot, rep_here, 1, 1)
    outgoing = jnp.einsum(
        "dks,sbc->dkbc",
        my_slot.astype(jnp.bfloat16),
        spill_cache,
        preferred_element_type=jnp.float32,
    ).astype(jnp.bfloat16)
    half = lax.all_to_all(outgoing, "attn", split_axis=0, concat_axis=0, tiled=True)
    other = lax.ppermute(half, "rep", [(i, (i + 1) % n_rep) for i in range(n_rep)])
    first = jnp.where(rep_here == 0, half, other)
    second = jnp.where(rep_here == 0, other, half)
    incoming = jnp.concatenate([first, second], axis=1)
    mine_slot = (owner_dev[:, None, :] == attn_here) & (
        order_rank[:, None, :] == slot_ids[None, :, None]
    )
    present = jnp.any(mine_slot, axis=2).reshape(-1)
    request = jnp.sum(
        jnp.where(mine_slot, directory[:, None, :] - attn_here * req_count, 0), axis=2
    ).reshape(-1)
    spill_rows = incoming.reshape(n_attn * CAP * blk, row_width)

    query_rows = queries.reshape(req_count, 2, head_count, row_width)
    lengths = local_len[0]
    starts = jnp.cumsum(lengths) - lengths
    pos = jnp.arange(pool_rows)
    pool_ok = (pos[None, :] >= starts[:, None]) & (pos[None, :] < (starts + lengths)[:, None])
    pool_scores = (
        jnp.einsum("rthc,kc->rthk", query_rows, cache_pool, preferred_element_type=jnp.float32)
        * score_scale
    )
    pool_scores = jnp.where(pool_ok[:, None, None, :], pool_scores, floor_score)
    fresh_scores = (
        jnp.einsum("rthc,kc->rthk", query_rows, new_latent, preferred_element_type=jnp.float32)
        * score_scale
    )
    fresh_pos = jnp.arange(2 * req_count)
    fresh_ok = (fresh_pos[None, None, :] // 2 == jnp.arange(req_count)[:, None, None]) & (
        fresh_pos[None, None, :] % 2 <= jnp.arange(2)[None, :, None]
    )
    fresh_scores = jnp.where(fresh_ok[:, :, None, :], fresh_scores, floor_score)
    block_ok = (request[None, :] == jnp.arange(req_count)[:, None]) & present[None, :]
    spill_ok = jnp.broadcast_to(block_ok[:, :, None], block_ok.shape + (blk,)).reshape(
        req_count, -1
    )
    spill_scores = (
        jnp.einsum("rthc,kc->rthk", query_rows, spill_rows, preferred_element_type=jnp.float32)
        * score_scale
    )
    spill_scores = jnp.where(spill_ok[:, None, None, :], spill_scores, floor_score)
    row_top = jnp.maximum(
        jnp.maximum(jnp.max(pool_scores, axis=3), jnp.max(fresh_scores, axis=3)),
        jnp.max(spill_scores, axis=3),
    )
    pool_weight = jnp.exp(pool_scores - row_top[..., None])
    fresh_weight = jnp.exp(fresh_scores - row_top[..., None])
    spill_weight = jnp.exp(spill_scores - row_top[..., None])
    denominator = (
        jnp.sum(pool_weight, axis=3) + jnp.sum(fresh_weight, axis=3) + jnp.sum(spill_weight, axis=3)
    )
    numerator = jnp.einsum(
        "rthk,kc->rthc",
        pool_weight.astype(jnp.bfloat16),
        cache_pool[:, :lat_width],
        preferred_element_type=jnp.float32,
    )
    numerator = numerator + jnp.einsum(
        "rthk,kc->rthc",
        fresh_weight.astype(jnp.bfloat16),
        new_latent[:, :lat_width],
        preferred_element_type=jnp.float32,
    )
    numerator = numerator + jnp.einsum(
        "rthk,kc->rthc",
        spill_weight.astype(jnp.bfloat16),
        spill_rows[:, :lat_width],
        preferred_element_type=jnp.float32,
    )
    attended = (numerator / denominator[..., None]).astype(jnp.bfloat16)
    values = jnp.einsum(
        "rthc,hcv->rthv", attended, w_uv, preferred_element_type=jnp.float32
    ).astype(jnp.bfloat16)
    tok_here = 2 * req_count
    values = values.reshape(tok_here, head_count * w_uv.shape[2])

    spread = jnp.broadcast_to(values[None], (n_attn,) + values.shape)
    all_values = lax.all_to_all(spread, "attn", split_axis=0, concat_axis=0, tiled=True)
    all_values = all_values.reshape(n_attn * tok_here, -1)
    partial_cols = jnp.dot(all_values, w_o, preferred_element_type=jnp.float32)

    tokens = partial_cols.shape[0]
    rows_part = tokens // n_rep
    sub_cols = partial_cols.shape[1] // n_expert
    pieces = (
        partial_cols.astype(jnp.bfloat16)
        .reshape(n_rep, rows_part, n_expert, sub_cols)
        .transpose(2, 0, 1, 3)
        .reshape(n_expert * n_rep, rows_part, sub_cols)
    )
    got = lax.all_to_all(pieces, ("expert", "rep"), split_axis=0, concat_axis=0, tiled=True)
    attn_own = jnp.sum(got.astype(jnp.float32), axis=0)
    res_own = lax.dynamic_slice(
        residual, (rep_here * rows_part, expert_here * sub_cols), (rows_part, sub_cols)
    )
    hidden_own = (res_own.astype(jnp.float32) + attn_own).astype(jnp.bfloat16)

    capacity = rows_part * TOP // EXPERTS * 5 // 4
    shards = n_attn * n_expert // EXPERTS
    pick, route_part = expert_tables(route_ids, rep_here, n_rep, capacity)
    pick_f = pick.astype(jnp.float32)
    rows_e = jnp.einsum(
        "jsr,rc->jsc", pick.astype(jnp.bfloat16), hidden_own, preferred_element_type=jnp.float32
    ).astype(jnp.bfloat16)
    send_rows = jnp.repeat(rows_e, shards, axis=0)
    recv_rows = lax.all_to_all(send_rows, ("attn", "expert"), split_axis=0, concat_axis=0, tiled=True)
    n_src = recv_rows.shape[0]
    widened = recv_rows.astype(jnp.float32)
    mean_sq = jnp.sum(widened * widened, axis=(0, 2)) / (n_src * sub_cols)
    inv = lax.rsqrt(mean_sq + 1e-06)
    normed = (
        widened * inv[None, :, None] * norm_gain.reshape(n_src, 1, sub_cols)
    ).astype(jnp.bfloat16)
    gate_blocks = w_gate.reshape(n_src, sub_cols, w_gate.shape[1])
    up_blocks = w_up.reshape(n_src, sub_cols, w_up.shape[1])
    gate_proj = jnp.einsum("skc,scu->ku", normed, gate_blocks, preferred_element_type=jnp.float32)
    up_proj = jnp.einsum("skc,scu->ku", normed, up_blocks, preferred_element_type=jnp.float32)
    activated = (jax.nn.silu(gate_proj) * up_proj).astype(jnp.bfloat16)
    n_dev = n_attn * n_expert
    down_blocks = w_down.reshape(w_down.shape[0], n_dev, sub_cols).transpose(1, 0, 2)
    back = jnp.einsum(
        "ku,duc->dkc", activated, down_blocks, preferred_element_type=jnp.float32
    ).astype(jnp.bfloat16)
    pack = (2, capacity * sub_cols // 2)
    returned = lax.all_to_all(
        back.reshape((n_dev,) + pack), ("attn", "expert"), split_axis=0, concat_axis=0, tiled=True
    )
    summed = jnp.sum(returned.astype(jnp.float32).reshape((EXPERTS, shards) + pack), axis=1)
    summed = summed.reshape(EXPERTS, capacity, sub_cols)
    share_part = lax.dynamic_slice_in_dim(route_scores, rep_here * rows_part, rows_part, 0)
    share_part = share_part / jnp.sum(share_part, axis=1, keepdims=True)
    share_table = jnp.sum(
        jnp.where(
            route_part[:, :, None] == jnp.arange(EXPERTS, dtype=jnp.int32)[None, None, :],
            share_part[:, :, None],
            0.0,
        ),
        axis=1,
    )
    coef = jnp.sum(jnp.where(pick, share_table.T[:, None, :], 0.0), axis=2) * scale_out
    weighted = coef[:, :, None] * summed
    routed = jnp.einsum("jsr,jsc->rc", pick_f, weighted, precision=HIGH)
    return (hidden_own.astype(jnp.float32) + routed).astype(jnp.bfloat16)


def solution(mesh):
    return jax.shard_map(
        per_device,
        mesh=mesh,
        in_specs=(
            P("attn", ("expert", "rep")),
            P("attn", None),
            P("attn", None),
            P("attn", None),
            P("attn", None, None),
            P(),
            P(("expert", "rep"), None, None),
            P(("expert", "rep"), "attn"),
            P(None, "attn"),
            P(),
            P(),
            P(),
            P(None, ("attn", "expert")),
            P(None, ("attn", "expert")),
            P(("attn", "expert"), None),
        ),
        out_specs=P("rep", ("attn", "expert")),
        check_vma=False,
    )
```

```python
import jax
import jax.numpy as jnp
from jax import lax
from jax.sharding import PartitionSpec as P

ROPE = 64
VH = 128
EXPERTS = 16
TOP = 4
CAP = 2


floor_score = -1e30
scale_out = 2.5
HIGH = lax.Precision.HIGHEST


def expert_tables(route_ids, part_index, part_count, capacity):
    row_count = route_ids.shape[0] // part_count
    route_part = lax.dynamic_slice_in_dim(route_ids, part_index * row_count, row_count, 0)
    member = jnp.any(
        route_part[:, :, None] == jnp.arange(EXPERTS, dtype=jnp.int32)[None, None, :], axis=1
    )
    order_rank = jnp.cumsum(member.astype(jnp.int32), axis=0) - 1
    slot_ids = jnp.arange(capacity, dtype=jnp.int32)
    pick = (member.T[:, None, :]) & (order_rank.T[:, None, :] == slot_ids[None, :, None])
    return pick, route_part


def per_device(
    queries,
    new_latent,
    cache_pool,
    local_len,
    spill_cache,
    spill_owner,
    w_uv,
    w_o,
    residual,
    norm_gain,
    route_ids,
    route_scores,
    w_gate,
    w_up,
    w_down,
):
    n_attn = lax.axis_size("attn")
    n_expert = lax.axis_size("expert")
    n_rep = lax.axis_size("rep")
    attn_here = lax.axis_index("attn")
    expert_here = lax.axis_index("expert")
    rep_here = lax.axis_index("rep")
    req_count = local_len.shape[1]
    head_count = w_uv.shape[0]
    row_width = new_latent.shape[1]
    lat_width = w_uv.shape[1]
    pool_rows = cache_pool.shape[0]
    score_scale = float(VH + ROPE) ** (-0.5)

    spill_count = spill_cache.shape[0]
    blk = spill_cache.shape[1]
    earlier = jnp.arange(spill_count)[:, None] > jnp.arange(spill_count)[None, :]
    own_ids = lax.dynamic_slice_in_dim(spill_owner, attn_here * spill_count, spill_count, 0)
    own_row = jnp.where(own_ids >= 0, own_ids // req_count, -1)
    own_rank = jnp.sum((own_row[:, None] == own_row[None, :]) & earlier, axis=1)
    my_slot = (own_row[None, :] == jnp.arange(n_attn)[:, None]) & (own_rank == rep_here)[None, :]
    outgoing = jnp.einsum(
        "ds,sbc->dbc",
        my_slot.astype(jnp.bfloat16),
        spill_cache,
        preferred_element_type=jnp.float32,
    ).astype(jnp.bfloat16)[:, None]
    half = lax.all_to_all(outgoing, "attn", split_axis=0, concat_axis=0, tiled=True)
    other = lax.ppermute(half, "rep", [(i, (i + 1) % n_rep) for i in range(n_rep)])
    incoming = jnp.concatenate([half, other], axis=1)
    directory = spill_owner.reshape(n_attn, spill_count)
    owner_dev = jnp.where(directory >= 0, directory // req_count, -1)
    same_owner = owner_dev[:, :, None] == owner_dev[:, None, :]
    order_rank = jnp.sum(same_owner & earlier[None, :, :], axis=2)
    slot_ids = jnp.stack([rep_here, n_rep - 1 - rep_here])
    mine_slot = (owner_dev[:, None, :] == attn_here) & (
        order_rank[:, None, :] == slot_ids[None, :, None]
    )
    present = jnp.any(mine_slot, axis=2).reshape(-1)
    request = jnp.sum(
        jnp.where(mine_slot, directory[:, None, :] - attn_here * req_count, 0), axis=2
    ).reshape(-1)
    spill_rows = incoming.reshape(n_attn * CAP * blk, row_width)

    query_rows = queries.reshape(req_count, 2, head_count, row_width)
    lengths = local_len[0]
    starts = jnp.cumsum(lengths) - lengths
    pos = jnp.arange(pool_rows)
    pool_ok = (pos[None, :] >= starts[:, None]) & (pos[None, :] < (starts + lengths)[:, None])
    pool_scores = (
        jnp.einsum("rthc,kc->rthk", query_rows, cache_pool, preferred_element_type=jnp.float32)
        * score_scale
    )
    pool_scores = jnp.where(pool_ok[:, None, None, :], pool_scores, floor_score)
    fresh_scores = (
        jnp.einsum("rthc,kc->rthk", query_rows, new_latent, preferred_element_type=jnp.float32)
        * score_scale
    )
    fresh_pos = jnp.arange(2 * req_count)
    fresh_ok = (fresh_pos[None, None, :] // 2 == jnp.arange(req_count)[:, None, None]) & (
        fresh_pos[None, None, :] % 2 <= jnp.arange(2)[None, :, None]
    )
    fresh_scores = jnp.where(fresh_ok[:, :, None, :], fresh_scores, floor_score)
    block_ok = (request[None, :] == jnp.arange(req_count)[:, None]) & present[None, :]
    spill_ok = jnp.broadcast_to(block_ok[:, :, None], block_ok.shape + (blk,)).reshape(
        req_count, -1
    )
    spill_scores = (
        jnp.einsum("rthc,kc->rthk", query_rows, spill_rows, preferred_element_type=jnp.float32)
        * score_scale
    )
    spill_scores = jnp.where(spill_ok[:, None, None, :], spill_scores, floor_score)
    row_top = jnp.maximum(
        jnp.maximum(jnp.max(pool_scores, axis=3), jnp.max(fresh_scores, axis=3)),
        jnp.max(spill_scores, axis=3),
    )
    pool_weight = jnp.exp(pool_scores - row_top[..., None])
    fresh_weight = jnp.exp(fresh_scores - row_top[..., None])
    spill_weight = jnp.exp(spill_scores - row_top[..., None])
    denominator = (
        jnp.sum(pool_weight, axis=3) + jnp.sum(fresh_weight, axis=3) + jnp.sum(spill_weight, axis=3)
    )
    numerator = jnp.einsum(
        "rthk,kc->rthc",
        pool_weight.astype(jnp.bfloat16),
        cache_pool[:, :lat_width],
        preferred_element_type=jnp.float32,
    )
    numerator = numerator + jnp.einsum(
        "rthk,kc->rthc",
        fresh_weight.astype(jnp.bfloat16),
        new_latent[:, :lat_width],
        preferred_element_type=jnp.float32,
    )
    numerator = numerator + jnp.einsum(
        "rthk,kc->rthc",
        spill_weight.astype(jnp.bfloat16),
        spill_rows[:, :lat_width],
        preferred_element_type=jnp.float32,
    )
    attended = (numerator / denominator[..., None]).astype(jnp.bfloat16)
    values = jnp.einsum(
        "rthc,hcv->rthv", attended, w_uv, preferred_element_type=jnp.float32
    ).astype(jnp.bfloat16)
    tok_here = 2 * req_count
    values = values.reshape(tok_here, head_count * w_uv.shape[2])

    spread = jnp.broadcast_to(values[None], (n_attn,) + values.shape)
    all_values = lax.all_to_all(spread, "attn", split_axis=0, concat_axis=0, tiled=True)
    all_values = all_values.reshape(n_attn * tok_here, -1)
    partial_cols = jnp.dot(all_values, w_o, preferred_element_type=jnp.float32)

    tokens = partial_cols.shape[0]
    rows_part = tokens // n_rep
    sub_cols = partial_cols.shape[1] // n_expert
    pieces = (
        partial_cols.astype(jnp.bfloat16)
        .reshape(n_rep, rows_part, n_expert, sub_cols)
        .transpose(2, 0, 1, 3)
        .reshape(n_expert * n_rep, rows_part, sub_cols)
    )
    got = lax.all_to_all(pieces, ("expert", "rep"), split_axis=0, concat_axis=0, tiled=True)
    attn_own = jnp.sum(got.astype(jnp.float32), axis=0)
    res_own = lax.dynamic_slice(
        residual, (rep_here * rows_part, expert_here * sub_cols), (rows_part, sub_cols)
    )
    hidden_own = (res_own.astype(jnp.float32) + attn_own).astype(jnp.bfloat16)

    capacity = rows_part * TOP // EXPERTS * 5 // 4
    shards = n_attn * n_expert // EXPERTS
    pick, route_part = expert_tables(route_ids, rep_here, n_rep, capacity)
    pick_f = pick.astype(jnp.float32)
    rows_e = jnp.einsum(
        "jsr,rc->jsc", pick.astype(jnp.bfloat16), hidden_own, preferred_element_type=jnp.float32
    ).astype(jnp.bfloat16)
    send_rows = jnp.repeat(rows_e, shards, axis=0)
    recv_rows = lax.all_to_all(send_rows, ("attn", "expert"), split_axis=0, concat_axis=0, tiled=True)
    n_src = recv_rows.shape[0]
    widened = recv_rows.astype(jnp.float32)
    mean_sq = jnp.sum(widened * widened, axis=(0, 2)) / (n_src * sub_cols)
    inv = lax.rsqrt(mean_sq + 1e-06)
    normed = (
        widened * inv[None, :, None] * norm_gain.reshape(n_src, 1, sub_cols)
    ).astype(jnp.bfloat16)
    gate_blocks = w_gate.reshape(n_src, sub_cols, w_gate.shape[1])
    up_blocks = w_up.reshape(n_src, sub_cols, w_up.shape[1])
    gate_proj = jnp.einsum("skc,scu->ku", normed, gate_blocks, preferred_element_type=jnp.float32)
    up_proj = jnp.einsum("skc,scu->ku", normed, up_blocks, preferred_element_type=jnp.float32)
    activated = (jax.nn.silu(gate_proj) * up_proj).astype(jnp.bfloat16)
    n_dev = n_attn * n_expert
    down_blocks = w_down.reshape(w_down.shape[0], n_dev, sub_cols).transpose(1, 0, 2)
    back = jnp.einsum(
        "ku,duc->dkc", activated, down_blocks, preferred_element_type=jnp.float32
    ).astype(jnp.bfloat16)
    pack = (2, capacity * sub_cols // 2)
    returned = lax.all_to_all(
        back.reshape((n_dev,) + pack), ("attn", "expert"), split_axis=0, concat_axis=0, tiled=True
    )
    summed = jnp.sum(returned.astype(jnp.float32).reshape((EXPERTS, shards) + pack), axis=1)
    summed = summed.reshape(EXPERTS, capacity, sub_cols)
    share_part = lax.dynamic_slice_in_dim(route_scores, rep_here * rows_part, rows_part, 0)
    share_part = share_part / jnp.sum(share_part, axis=1, keepdims=True)
    share_table = jnp.sum(
        jnp.where(
            route_part[:, :, None] == jnp.arange(EXPERTS, dtype=jnp.int32)[None, None, :],
            share_part[:, :, None],
            0.0,
        ),
        axis=1,
    )
    coef = jnp.sum(jnp.where(pick, share_table.T[:, None, :], 0.0), axis=2) * scale_out
    weighted = coef[:, :, None] * summed
    routed = jnp.einsum("jsr,jsc->rc", pick_f, weighted, precision=HIGH)
    return (hidden_own.astype(jnp.float32) + routed).astype(jnp.bfloat16)


def solution(mesh):
    return jax.shard_map(
        per_device,
        mesh=mesh,
        in_specs=(
            P("attn", ("expert", "rep")),
            P("attn", None),
            P("attn", None),
            P("attn", None),
            P("attn", None, None),
            P(),
            P(("expert", "rep"), None, None),
            P(("expert", "rep"), "attn"),
            P(None, "attn"),
            P(),
            P(),
            P(),
            P(None, ("attn", "expert")),
            P(None, ("attn", "expert")),
            P(("attn", "expert"), None),
        ),
        out_specs=P("rep", ("attn", "expert")),
        check_vma=False,
    )
```

```python
import jax
import jax.numpy as jnp
from jax import lax
from jax.sharding import PartitionSpec as P

ROPE = 64
VH = 128
EXPERTS = 16
TOP = 4
CAP = 2


floor_score = -1e30
scale_out = 2.5
HIGH = lax.Precision.HIGHEST


def expert_tables(route_ids, part_index, part_count, capacity):
    row_count = route_ids.shape[0] // part_count
    route_part = lax.dynamic_slice_in_dim(route_ids, part_index * row_count, row_count, 0)
    member = jnp.any(
        route_part[:, :, None] == jnp.arange(EXPERTS, dtype=jnp.int32)[None, None, :], axis=1
    )
    order_rank = jnp.cumsum(member.astype(jnp.int32), axis=0) - 1
    slot_ids = jnp.arange(capacity, dtype=jnp.int32)
    pick = (member.T[:, None, :]) & (order_rank.T[:, None, :] == slot_ids[None, :, None])
    return pick, route_part


def per_device(
    queries,
    new_latent,
    cache_pool,
    local_len,
    spill_cache,
    spill_owner,
    w_uv,
    w_o,
    residual,
    norm_gain,
    route_ids,
    route_scores,
    w_gate,
    w_up,
    w_down,
):
    n_attn = lax.axis_size("attn")
    n_expert = lax.axis_size("expert")
    n_rep = lax.axis_size("rep")
    attn_here = lax.axis_index("attn")
    expert_here = lax.axis_index("expert")
    rep_here = lax.axis_index("rep")
    req_count = local_len.shape[1]
    head_count = w_uv.shape[0]
    row_width = new_latent.shape[1]
    lat_width = w_uv.shape[1]
    pool_rows = cache_pool.shape[0]
    score_scale = float(VH + ROPE) ** (-0.5)

    spill_count = spill_cache.shape[0]
    blk = spill_cache.shape[1]
    earlier = jnp.arange(spill_count)[:, None] > jnp.arange(spill_count)[None, :]
    own_ids = lax.dynamic_slice_in_dim(spill_owner, attn_here * spill_count, spill_count, 0)
    own_row = jnp.where(own_ids >= 0, own_ids // req_count, -1)
    own_rank = jnp.sum((own_row[:, None] == own_row[None, :]) & earlier, axis=1)
    my_slot = (own_row[None, :] == jnp.arange(n_attn)[:, None]) & (own_rank == rep_here)[None, :]
    outgoing = jnp.einsum(
        "ds,sbc->dbc",
        my_slot.astype(jnp.bfloat16),
        spill_cache,
        preferred_element_type=jnp.float32,
    ).astype(jnp.bfloat16)[:, None]
    half = lax.all_to_all(outgoing, "attn", split_axis=0, concat_axis=0, tiled=True)
    other = lax.ppermute(half, "rep", [(i, (i + 1) % n_rep) for i in range(n_rep)])
    incoming = jnp.concatenate([half, other], axis=1)
    directory = spill_owner.reshape(n_attn, spill_count)
    owner_dev = jnp.where(directory >= 0, directory // req_count, -1)
    same_owner = owner_dev[:, :, None] == owner_dev[:, None, :]
    order_rank = jnp.sum(same_owner & earlier[None, :, :], axis=2)
    slot_ids = jnp.stack([rep_here, n_rep - 1 - rep_here])
    mine_slot = (owner_dev[:, None, :] == attn_here) & (
        order_rank[:, None, :] == slot_ids[None, :, None]
    )
    present = jnp.any(mine_slot, axis=2).reshape(-1)
    request = jnp.sum(
        jnp.where(mine_slot, directory[:, None, :] - attn_here * req_count, 0), axis=2
    ).reshape(-1)
    spill_rows = incoming.reshape(n_attn * CAP * blk, row_width)

    query_rows = queries.reshape(req_count, 2, head_count, row_width)
    lengths = local_len[0]
    starts = jnp.cumsum(lengths) - lengths
    pos = jnp.arange(pool_rows)
    pool_ok = (pos[None, :] >= starts[:, None]) & (pos[None, :] < (starts + lengths)[:, None])
    pool_scores = (
        jnp.einsum("rthc,kc->rthk", query_rows, cache_pool, preferred_element_type=jnp.float32)
        * score_scale
    )
    pool_scores = jnp.where(pool_ok[:, None, None, :], pool_scores, floor_score)
    fresh_scores = (
        jnp.einsum("rthc,kc->rthk", query_rows, new_latent, preferred_element_type=jnp.float32)
        * score_scale
    )
    fresh_pos = jnp.arange(2 * req_count)
    fresh_ok = (fresh_pos[None, None, :] // 2 == jnp.arange(req_count)[:, None, None]) & (
        fresh_pos[None, None, :] % 2 <= jnp.arange(2)[None, :, None]
    )
    fresh_scores = jnp.where(fresh_ok[:, :, None, :], fresh_scores, floor_score)
    block_ok = (request[None, :] == jnp.arange(req_count)[:, None]) & present[None, :]
    spill_ok = jnp.broadcast_to(block_ok[:, :, None], block_ok.shape + (blk,)).reshape(
        req_count, -1
    )
    spill_scores = (
        jnp.einsum("rthc,kc->rthk", query_rows, spill_rows, preferred_element_type=jnp.float32)
        * score_scale
    )
    spill_scores = jnp.where(spill_ok[:, None, None, :], spill_scores, floor_score)
    row_top = jnp.maximum(
        jnp.maximum(jnp.max(pool_scores, axis=3), jnp.max(fresh_scores, axis=3)),
        jnp.max(spill_scores, axis=3),
    )
    pool_weight = jnp.exp(pool_scores - row_top[..., None])
    fresh_weight = jnp.exp(fresh_scores - row_top[..., None])
    spill_weight = jnp.exp(spill_scores - row_top[..., None])
    denominator = (
        jnp.sum(pool_weight, axis=3) + jnp.sum(fresh_weight, axis=3) + jnp.sum(spill_weight, axis=3)
    )
    numerator = jnp.einsum(
        "rthk,kc->rthc",
        pool_weight.astype(jnp.bfloat16),
        cache_pool[:, :lat_width],
        preferred_element_type=jnp.float32,
    )
    numerator = numerator + jnp.einsum(
        "rthk,kc->rthc",
        fresh_weight.astype(jnp.bfloat16),
        new_latent[:, :lat_width],
        preferred_element_type=jnp.float32,
    )
    numerator = numerator + jnp.einsum(
        "rthk,kc->rthc",
        spill_weight.astype(jnp.bfloat16),
        spill_rows[:, :lat_width],
        preferred_element_type=jnp.float32,
    )
    attended = (numerator / denominator[..., None]).astype(jnp.bfloat16)
    values = jnp.einsum(
        "rthc,hcv->rthv", attended, w_uv, preferred_element_type=jnp.float32
    ).astype(jnp.bfloat16)
    tok_here = 2 * req_count
    values = values.reshape(tok_here, head_count * w_uv.shape[2])

    spread = jnp.broadcast_to(values[None], (n_attn,) + values.shape)
    all_values = lax.all_to_all(spread, "attn", split_axis=0, concat_axis=0, tiled=True)
    all_values = all_values.reshape(n_attn * tok_here, -1)
    partial_cols = jnp.dot(all_values, w_o, preferred_element_type=jnp.float32)

    tokens = partial_cols.shape[0]
    rows_part = tokens // n_rep
    sub_cols = partial_cols.shape[1] // n_expert
    pieces = (
        partial_cols.astype(jnp.bfloat16)
        .reshape(n_rep, rows_part, n_expert, sub_cols)
        .transpose(2, 0, 1, 3)
        .reshape(n_expert * n_rep, rows_part, sub_cols)
    )
    got = lax.all_to_all(pieces, ("expert", "rep"), split_axis=0, concat_axis=0, tiled=True)
    attn_own = jnp.sum(got.astype(jnp.float32), axis=0)
    res_own = lax.dynamic_slice(
        residual, (rep_here * rows_part, expert_here * sub_cols), (rows_part, sub_cols)
    )
    hidden_own = (res_own.astype(jnp.float32) + attn_own).astype(jnp.bfloat16)

    capacity = rows_part * TOP // EXPERTS * 5 // 4
    shards = n_attn * n_expert // EXPERTS
    pick, route_part = expert_tables(route_ids, rep_here, n_rep, capacity)
    pick_f = pick.astype(jnp.float32)
    rows_e = jnp.einsum(
        "jsr,rc->jsc", pick.astype(jnp.bfloat16), hidden_own, preferred_element_type=jnp.float32
    ).astype(jnp.bfloat16)
    send_rows = jnp.repeat(rows_e, shards, axis=0)
    recv_rows = lax.all_to_all(send_rows, ("attn", "expert"), split_axis=0, concat_axis=0, tiled=True)
    n_src = recv_rows.shape[0]
    widened = recv_rows.astype(jnp.float32)
    mean_sq = jnp.sum(widened * widened, axis=(0, 2)) / (n_src * sub_cols)
    inv = lax.rsqrt(mean_sq + 1e-06)
    normed = (
        widened * inv[None, :, None] * norm_gain.reshape(n_src, 1, sub_cols)
    ).astype(jnp.bfloat16)
    gate_blocks = w_gate.reshape(n_src, sub_cols, w_gate.shape[1])
    up_blocks = w_up.reshape(n_src, sub_cols, w_up.shape[1])
    gate_proj = jnp.einsum("skc,scu->ku", normed, gate_blocks, preferred_element_type=jnp.float32)
    up_proj = jnp.einsum("skc,scu->ku", normed, up_blocks, preferred_element_type=jnp.float32)
    activated = (jax.nn.silu(gate_proj) * up_proj).astype(jnp.bfloat16)
    n_dev = n_attn * n_expert
    per_attn = shards // n_expert
    down_blocks = (
        w_down.reshape(w_down.shape[0], n_attn, n_expert, sub_cols)
        .transpose(2, 1, 0, 3)
        .reshape(n_dev, w_down.shape[0], sub_cols)
    )
    back = jnp.einsum(
        "ku,duc->dkc", activated, down_blocks, preferred_element_type=jnp.float32
    ).astype(jnp.bfloat16)
    pack = (2, capacity * sub_cols // 2)
    returned = lax.all_to_all(
        back.reshape((n_dev,) + pack), ("expert", "attn"), split_axis=0, concat_axis=0, tiled=True
    )
    summed = jnp.sum(
        returned.astype(jnp.float32).reshape((n_expert, EXPERTS, per_attn) + pack), axis=(0, 2)
    )
    summed = summed.reshape(EXPERTS, capacity, sub_cols)
    share_part = lax.dynamic_slice_in_dim(route_scores, rep_here * rows_part, rows_part, 0)
    share_part = share_part / jnp.sum(share_part, axis=1, keepdims=True)
    share_table = jnp.sum(
        jnp.where(
            route_part[:, :, None] == jnp.arange(EXPERTS, dtype=jnp.int32)[None, None, :],
            share_part[:, :, None],
            0.0,
        ),
        axis=1,
    )
    coef = jnp.sum(jnp.where(pick, share_table.T[:, None, :], 0.0), axis=2) * scale_out
    weighted = coef[:, :, None] * summed
    routed = jnp.einsum("jsr,jsc->rc", pick_f, weighted, precision=HIGH)
    return (hidden_own.astype(jnp.float32) + routed).astype(jnp.bfloat16)


def solution(mesh):
    return jax.shard_map(
        per_device,
        mesh=mesh,
        in_specs=(
            P("attn", ("expert", "rep")),
            P("attn", None),
            P("attn", None),
            P("attn", None),
            P("attn", None, None),
            P(),
            P(("expert", "rep"), None, None),
            P(("expert", "rep"), "attn"),
            P(None, "attn"),
            P(),
            P(),
            P(),
            P(None, ("attn", "expert")),
            P(None, ("attn", "expert")),
            P(("attn", "expert"), None),
        ),
        out_specs=P("rep", ("attn", "expert")),
        check_vma=False,
    )
```

```python
import jax
import jax.numpy as jnp
from jax import lax
from jax.sharding import PartitionSpec as P

ROPE = 64
VH = 128
EXPERTS = 16
TOP = 4
CAP = 2


floor_score = -1e30
scale_out = 2.5
HIGH = lax.Precision.HIGHEST


def expert_tables(route_ids, part_index, part_count, capacity):
    row_count = route_ids.shape[0] // part_count
    route_part = lax.dynamic_slice_in_dim(route_ids, part_index * row_count, row_count, 0)
    member = jnp.any(
        route_part[:, :, None] == jnp.arange(EXPERTS, dtype=jnp.int32)[None, None, :], axis=1
    )
    order_rank = jnp.cumsum(member.astype(jnp.int32), axis=0) - 1
    slot_ids = jnp.arange(capacity, dtype=jnp.int32)
    pick = (member.T[:, None, :]) & (order_rank.T[:, None, :] == slot_ids[None, :, None])
    return pick, route_part


def per_device(
    queries,
    new_latent,
    cache_pool,
    local_len,
    spill_cache,
    spill_owner,
    w_uv,
    w_o,
    residual,
    norm_gain,
    route_ids,
    route_scores,
    w_gate,
    w_up,
    w_down,
):
    n_attn = lax.axis_size("attn")
    n_expert = lax.axis_size("expert")
    n_rep = lax.axis_size("rep")
    attn_here = lax.axis_index("attn")
    expert_here = lax.axis_index("expert")
    rep_here = lax.axis_index("rep")
    req_count = local_len.shape[1]
    head_count = w_uv.shape[0]
    row_width = new_latent.shape[1]
    lat_width = w_uv.shape[1]
    pool_rows = cache_pool.shape[0]
    score_scale = float(VH + ROPE) ** (-0.5)

    spill_count = spill_cache.shape[0]
    blk = spill_cache.shape[1]
    earlier = jnp.arange(spill_count)[:, None] > jnp.arange(spill_count)[None, :]
    own_ids = lax.dynamic_slice_in_dim(spill_owner, attn_here * spill_count, spill_count, 0)
    own_row = jnp.where(own_ids >= 0, own_ids // req_count, -1)
    own_rank = jnp.sum((own_row[:, None] == own_row[None, :]) & earlier, axis=1)
    my_slot = (own_row[None, :] == jnp.arange(n_attn)[:, None]) & (own_rank == rep_here)[None, :]
    outgoing = jnp.einsum(
        "ds,sbc->dbc",
        my_slot.astype(jnp.bfloat16),
        spill_cache,
        preferred_element_type=jnp.float32,
    ).astype(jnp.bfloat16)[:, None]
    half = lax.all_to_all(outgoing, "attn", split_axis=0, concat_axis=0, tiled=True)
    other = lax.ppermute(half, "rep", [(i, (i + 1) % n_rep) for i in range(n_rep)])
    incoming = jnp.concatenate([half, other], axis=1)
    directory = spill_owner.reshape(n_attn, spill_count)
    owner_dev = jnp.where(directory >= 0, directory // req_count, -1)
    same_owner = owner_dev[:, :, None] == owner_dev[:, None, :]
    order_rank = jnp.sum(same_owner & earlier[None, :, :], axis=2)
    slot_ids = jnp.stack([rep_here, n_rep - 1 - rep_here])
    mine_slot = (owner_dev[:, None, :] == attn_here) & (
        order_rank[:, None, :] == slot_ids[None, :, None]
    )
    present = jnp.any(mine_slot, axis=2).reshape(-1)
    request = jnp.sum(
        jnp.where(mine_slot, directory[:, None, :] - attn_here * req_count, 0), axis=2
    ).reshape(-1)
    spill_rows = incoming.reshape(n_attn * CAP * blk, row_width)

    query_rows = queries.reshape(req_count, 2, head_count, row_width)
    lengths = local_len[0]
    starts = jnp.cumsum(lengths) - lengths
    pos = jnp.arange(pool_rows)
    pool_ok = (pos[None, :] >= starts[:, None]) & (pos[None, :] < (starts + lengths)[:, None])
    pool_scores = (
        jnp.einsum("rthc,kc->rthk", query_rows, cache_pool, preferred_element_type=jnp.float32)
        * score_scale
    )
    pool_scores = jnp.where(pool_ok[:, None, None, :], pool_scores, floor_score)
    fresh_scores = (
        jnp.einsum("rthc,kc->rthk", query_rows, new_latent, preferred_element_type=jnp.float32)
        * score_scale
    )
    fresh_pos = jnp.arange(2 * req_count)
    fresh_ok = (fresh_pos[None, None, :] // 2 == jnp.arange(req_count)[:, None, None]) & (
        fresh_pos[None, None, :] % 2 <= jnp.arange(2)[None, :, None]
    )
    fresh_scores = jnp.where(fresh_ok[:, :, None, :], fresh_scores, floor_score)
    block_ok = (request[None, :] == jnp.arange(req_count)[:, None]) & present[None, :]
    spill_ok = jnp.broadcast_to(block_ok[:, :, None], block_ok.shape + (blk,)).reshape(
        req_count, -1
    )
    spill_scores = (
        jnp.einsum("rthc,kc->rthk", query_rows, spill_rows, preferred_element_type=jnp.float32)
        * score_scale
    )
    spill_scores = jnp.where(spill_ok[:, None, None, :], spill_scores, floor_score)
    row_top = jnp.maximum(
        jnp.maximum(jnp.max(pool_scores, axis=3), jnp.max(fresh_scores, axis=3)),
        jnp.max(spill_scores, axis=3),
    )
    pool_weight = jnp.exp(pool_scores - row_top[..., None])
    fresh_weight = jnp.exp(fresh_scores - row_top[..., None])
    spill_weight = jnp.exp(spill_scores - row_top[..., None])
    denominator = (
        jnp.sum(pool_weight, axis=3) + jnp.sum(fresh_weight, axis=3) + jnp.sum(spill_weight, axis=3)
    )
    numerator = jnp.einsum(
        "rthk,kc->rthc",
        pool_weight.astype(jnp.bfloat16),
        cache_pool[:, :lat_width],
        preferred_element_type=jnp.float32,
    )
    numerator = numerator + jnp.einsum(
        "rthk,kc->rthc",
        fresh_weight.astype(jnp.bfloat16),
        new_latent[:, :lat_width],
        preferred_element_type=jnp.float32,
    )
    numerator = numerator + jnp.einsum(
        "rthk,kc->rthc",
        spill_weight.astype(jnp.bfloat16),
        spill_rows[:, :lat_width],
        preferred_element_type=jnp.float32,
    )
    attended = (numerator / denominator[..., None]).astype(jnp.bfloat16)
    values = jnp.einsum(
        "rthc,hcv->rthv", attended, w_uv, preferred_element_type=jnp.float32
    ).astype(jnp.bfloat16)
    tok_here = 2 * req_count
    values = values.reshape(tok_here, head_count * w_uv.shape[2])

    spread = jnp.broadcast_to(values[None], (n_attn,) + values.shape)
    all_values = lax.all_to_all(spread, "attn", split_axis=0, concat_axis=0, tiled=True)
    all_values = all_values.reshape(n_attn * tok_here, -1)
    partial_cols = jnp.dot(all_values, w_o, preferred_element_type=jnp.float32)

    tokens = partial_cols.shape[0]
    rows_part = tokens // n_rep
    sub_cols = partial_cols.shape[1] // n_expert
    pieces = (
        partial_cols.astype(jnp.bfloat16)
        .reshape(n_rep, rows_part, n_expert, sub_cols)
        .transpose(2, 0, 1, 3)
        .reshape(n_expert * n_rep, rows_part, sub_cols)
    )
    got = lax.all_to_all(pieces, ("expert", "rep"), split_axis=0, concat_axis=0, tiled=True)
    attn_own = jnp.sum(got.astype(jnp.float32), axis=0)
    res_own = lax.dynamic_slice(
        residual, (rep_here * rows_part, expert_here * sub_cols), (rows_part, sub_cols)
    )
    hidden_own = (res_own.astype(jnp.float32) + attn_own).astype(jnp.bfloat16)

    capacity = rows_part * TOP // EXPERTS * 5 // 4
    shards = n_attn * n_expert // EXPERTS
    pick, route_part = expert_tables(route_ids, rep_here, n_rep, capacity)
    pick_f = pick.astype(jnp.float32)
    rows_e = jnp.einsum(
        "jsr,rc->jsc", pick.astype(jnp.bfloat16), hidden_own, preferred_element_type=jnp.float32
    ).astype(jnp.bfloat16)
    per_attn = shards // n_expert
    send_rows = jnp.broadcast_to(
        rows_e[None, :, None], (n_expert, EXPERTS, per_attn) + rows_e.shape[1:]
    ).reshape((-1,) + rows_e.shape[1:])
    recv_rows = lax.all_to_all(send_rows, ("expert", "attn"), split_axis=0, concat_axis=0, tiled=True)
    n_src = recv_rows.shape[0]
    widened = recv_rows.astype(jnp.float32).reshape(n_expert, n_attn, capacity, sub_cols)
    mean_sq = jnp.sum(widened * widened, axis=(0, 1, 3)) / (n_src * sub_cols)
    inv = lax.rsqrt(mean_sq + 1e-06)
    gain = norm_gain.reshape(n_attn, n_expert, sub_cols).swapaxes(0, 1)[:, :, None, :]
    normed = (widened * inv[None, None, :, None] * gain).astype(jnp.bfloat16)
    gate_blocks = w_gate.reshape(n_attn, n_expert, sub_cols, w_gate.shape[1])
    up_blocks = w_up.reshape(n_attn, n_expert, sub_cols, w_up.shape[1])
    gate_proj = jnp.einsum("eakc,aecu->ku", normed, gate_blocks, preferred_element_type=jnp.float32)
    up_proj = jnp.einsum("eakc,aecu->ku", normed, up_blocks, preferred_element_type=jnp.float32)
    activated = (jax.nn.silu(gate_proj) * up_proj).astype(jnp.bfloat16)
    n_dev = n_attn * n_expert
    down_blocks = (
        w_down.reshape(w_down.shape[0], n_attn, n_expert, sub_cols)
        .transpose(2, 1, 0, 3)
        .reshape(n_dev, w_down.shape[0], sub_cols)
    )
    back = jnp.einsum(
        "ku,duc->dkc", activated, down_blocks, preferred_element_type=jnp.float32
    ).astype(jnp.bfloat16)
    pack = (2, capacity * sub_cols // 2)
    returned = lax.all_to_all(
        back.reshape((n_dev,) + pack), ("expert", "attn"), split_axis=0, concat_axis=0, tiled=True
    )
    summed = jnp.sum(
        returned.astype(jnp.float32).reshape((n_expert, EXPERTS, per_attn) + pack), axis=(0, 2)
    )
    summed = summed.reshape(EXPERTS, capacity, sub_cols)
    share_part = lax.dynamic_slice_in_dim(route_scores, rep_here * rows_part, rows_part, 0)
    share_part = share_part / jnp.sum(share_part, axis=1, keepdims=True)
    share_table = jnp.sum(
        jnp.where(
            route_part[:, :, None] == jnp.arange(EXPERTS, dtype=jnp.int32)[None, None, :],
            share_part[:, :, None],
            0.0,
        ),
        axis=1,
    )
    coef = jnp.sum(jnp.where(pick, share_table.T[:, None, :], 0.0), axis=2) * scale_out
    weighted = coef[:, :, None] * summed
    routed = jnp.einsum("jsr,jsc->rc", pick_f, weighted, precision=HIGH)
    return (hidden_own.astype(jnp.float32) + routed).astype(jnp.bfloat16)


def solution(mesh):
    return jax.shard_map(
        per_device,
        mesh=mesh,
        in_specs=(
            P("attn", ("expert", "rep")),
            P("attn", None),
            P("attn", None),
            P("attn", None),
            P("attn", None, None),
            P(),
            P(("expert", "rep"), None, None),
            P(("expert", "rep"), "attn"),
            P(None, "attn"),
            P(),
            P(),
            P(),
            P(None, ("attn", "expert")),
            P(None, ("attn", "expert")),
            P(("attn", "expert"), None),
        ),
        out_specs=P("rep", ("attn", "expert")),
        check_vma=False,
    )
```
